512 devices in a mesh: dom: 64 (over z_hi, y, core), cls: 8 (over z_lo, x).
Axes of the slice: x: 4, y: 8, z: 8 (z_hi: 4, z_lo: 2; z = z_hi * 2 + z_lo), core: 2. Of those that a mesh axis runs over, the one named last changes fastest.
Arguments:
- particles: bfloat16 [512, 64, 64], P(('dom', 'cls')), as said below
- group_ids: int32 [512], P(('dom', 'cls')), may hold values from 0 to 15
- references: float32 [96, 4096], P('cls', 'dom'), as said below
- ctf_profile: float32 [16, 23], replicated, may hold values from 0.1 to 1
- noise_power: float32 [23], replicated, may hold values from 2 to 16
Outputs:
- new_refs: float32 [2, 96, 1024], P(None, 'cls', 'dom')
- log_evidence: float32 [512], P('dom')
The draws below stay inside these ranges and needn't reach their ends.
Inputs may be any that keep to these rules, and one draw needn't show every extreme that they name: `particles`: pixel values. `references`: pixel values.
All inputs are finite; a program needn't handle non-finite values.
Results may differ from the reference program's by a relative error of at most 0.011.
Values may be sent and summed in bfloat16 or wider, within the bound.
No kernel may reach another device: no remote copies, remote signals or barrier semaphores. Data moves between devices by JAX's collectives and lax.ppermute only.
A program may use at most 64 MiB of HBM per device.

```python
import math
import jax
import jax.numpy as jnp
from jax import lax

L = 64
BAND = 32
ROT = 8
NRAD = 23
GROUPS = 16
K = 96
P_TOT = 512


def class_maps(key):
    return jnp.clip(jax.random.normal(jax.random.fold_in(key, 11), (K, L * L), jnp.float32), -5.0, 5.0)


def draw_references(key, part):
    return class_maps(key)


def draw_particles(key, part):
    values = jax.random.normal(jax.random.fold_in(key, 14), (P_TOT, L, L), jnp.float32)
    return jnp.clip(values, -16.0, 16.0).astype(jnp.bfloat16)


def set_ends(entries, rng, smallest, largest):
    extent = entries.shape
    spot = [jax.random.randint(jax.random.fold_in(rng, axis), (), 0, extent[axis]) for axis in range(len(extent))]
    entries = entries.at[tuple(spot)].set(smallest)
    longest = extent.index(max(extent))
    spot[longest] = (spot[longest] + 1) % extent[longest]
    return entries.at[tuple(spot)].set(largest)


def setup_inputs(seed: int = 0) -> dict:
    key_list = jax.random.split(jax.random.key(seed), 6)
    return {
        "particles": draw_particles(jax.random.fold_in(key_list[5], 71), 0),
        "group_ids": set_ends(jax.random.randint(key_list[1], (P_TOT,), 0, GROUPS), jax.random.fold_in(key_list[1], 1), 0, GROUPS - 1).astype(jnp.int32),
        "references": draw_references(jax.random.fold_in(key_list[5], 71), 0),
        "ctf_profile": jnp.clip(jax.random.uniform(key_list[3], (GROUPS, NRAD), jnp.float32, 0.1, 1.0), 0.1, 1.0),
        "noise_power": jnp.clip(jnp.exp(jax.random.uniform(key_list[4], (NRAD,), jnp.float32, math.log(2.0), math.log(16.0))), 2.0, 16.0),
    }


HIGHEST = lax.Precision.HIGHEST


def phase_tables(size, band):
    pixel = jnp.arange(size, dtype=jnp.int32)
    freq = jnp.arange(band, dtype=jnp.int32) - band // 2
    turned = (freq[:, None] * pixel[None, :]) % size
    angle = turned.astype(jnp.float32) * (2.0 * math.pi / size)
    return jnp.cos(angle), jnp.sin(angle)


def forward_tables(cosine, sine):
    fcos = cosine / 8.0
    fsin = sine / 8.0
    first_table_part = jnp.stack([fcos.T, -fsin.T], axis=1)
    second_table_part = jnp.stack([jnp.stack([fcos.T, -fsin.T], axis=1), jnp.stack([fsin.T, fcos.T], axis=1)], axis=1)
    return first_table_part, second_table_part


def inverse_tables(cosine, sine):
    icos = cosine.astype(jnp.bfloat16)
    isin = sine.astype(jnp.bfloat16)
    tab_c = jnp.stack([jnp.stack([icos, isin], axis=1), jnp.stack([-isin, icos], axis=1)], axis=0)
    tab_d = jnp.stack([icos, -isin], axis=0)
    tab_e = jnp.stack([icos.T, isin.T], axis=1)
    tab_f = jnp.stack([jnp.stack([icos.T, isin.T], axis=1), jnp.stack([-isin.T, icos.T], axis=1)], axis=1)
    return tab_c, tab_d, tab_e, tab_f


def product(form, left, right):
    return jnp.einsum(form, left.astype(jnp.float32), right.astype(jnp.float32))


def orient(images):
    turned = jnp.swapaxes(images, 1, 2)
    views = [jnp.rot90(images, j, axes=(1, 2)) for j in range(4)]
    views = views + [jnp.rot90(turned, j, axes=(1, 2)) for j in range(4)]
    return jnp.stack(views, axis=1)


def particle_band_rows(images, first_table_part, second_table_part):
    count = images.shape[0]
    oriented = orient(images)
    half = product("nryx,xdb->nrydb", oriented, first_table_part).astype(jnp.bfloat16)
    full = product("nrydb,ydca->nrcab", half, second_table_part).astype(jnp.bfloat16)
    return full.reshape(count, ROT, 2, BAND * BAND)


def class_bands(maps, first_table_part, second_table_part):
    count = maps.shape[0]
    images = maps.reshape(count, L, L)
    half = jnp.einsum("kyx,xdb->kydb", images, first_table_part, precision=HIGHEST)
    full = jnp.einsum("kydb,ydca->kcab", half, second_table_part, precision=HIGHEST)
    return full.reshape(count, 2, BAND * BAND)


def spectra(ctf_profile, noise_power, group_ids):
    freq = jnp.arange(BAND, dtype=jnp.int32) - BAND // 2
    square = (freq[:, None] ** 2 + freq[None, :] ** 2).reshape(-1)
    bounds = jnp.arange(1, NRAD, dtype=jnp.int32) ** 2
    shell = jnp.sum((square[None, :] >= bounds[:, None]).astype(jnp.int32), axis=0)
    shells = (shell[None, :] == jnp.arange(NRAD, dtype=jnp.int32)[:, None]).astype(jnp.float32)
    groups = (group_ids[:, None] == jnp.arange(GROUPS, dtype=jnp.int32)[None, :]).astype(jnp.float32)
    profile = jnp.dot(groups, ctf_profile, precision=HIGHEST)
    contrast_transfer = jnp.dot(profile, shells, precision=HIGHEST)
    noise_deviation = jnp.dot(noise_power, shells, precision=HIGHEST)
    return contrast_transfer, noise_deviation


def class_step(abstract_value, output_value, ref_band, offset, tabs):
    tab_c, tab_d, tab_e, tab_f = tabs
    count = abstract_value.shape[0]
    real_ref = ref_band[0]
    imag_ref = ref_band[1]
    breal = abstract_value[:, :, 0] * real_ref + abstract_value[:, :, 1] * imag_ref
    bimag = abstract_value[:, :, 1] * real_ref - abstract_value[:, :, 0] * imag_ref
    bmat = jnp.stack([breal, bimag], axis=2).astype(jnp.bfloat16).reshape(count, ROT, 2, BAND, BAND)
    edge = product("nrcab,cbdx->nradx", bmat, tab_c).astype(jnp.bfloat16)
    score = product("nradx,day->nyrx", edge, tab_d) - offset[:, None, None, None]
    peak = jnp.max(score, axis=(1, 2, 3))
    expo = jnp.exp(score - peak[:, None, None, None])
    total = jnp.sum(expo, axis=(1, 2, 3))
    uhalf = product("nyrx,xdb->nrydb", expo.astype(jnp.bfloat16), tab_e).astype(jnp.bfloat16)
    what = product("nrydb,ydca->nrcab", uhalf, tab_f).astype(jnp.bfloat16)
    what = what.reshape(count, ROT, 2, BAND * BAND).astype(jnp.float32)
    preal = jnp.sum(output_value[:, :, 0] * what[:, :, 0] - output_value[:, :, 1] * what[:, :, 1], axis=1)
    pimag = jnp.sum(output_value[:, :, 0] * what[:, :, 1] + output_value[:, :, 1] * what[:, :, 0], axis=1)
    return peak, total, jnp.stack([preal, pimag], axis=1)


def reference(particles, group_ids, references, ctf_profile, noise_power):
    cosine, sine = phase_tables(L, BAND)
    first_table_part, second_table_part = forward_tables(cosine, sine)
    tabs = inverse_tables(cosine, sine)
    fourier_input = particle_band_rows(particles, first_table_part.astype(jnp.bfloat16), second_table_part.astype(jnp.bfloat16)).astype(jnp.float32)
    contrast_transfer, noise_deviation = spectra(ctf_profile, noise_power, group_ids)
    abstract_value = fourier_input * (contrast_transfer / noise_deviation[None, :])[:, None, None, :]
    output_value = fourier_input * contrast_transfer[:, None, None, :]
    rbands = class_bands(references, first_table_part, second_table_part)
    power = rbands[:, 0] ** 2 + rbands[:, 1] ** 2
    offset = 0.5 * jnp.dot(contrast_transfer * contrast_transfer / noise_deviation[None, :], power.T, precision=HIGHEST)
    peaks, totals, projs = lax.map(lambda item: class_step(abstract_value, output_value, item[0], item[1], tabs), (rbands, offset.T))
    top = jnp.max(peaks, axis=0)
    mass = jnp.sum(jnp.exp(peaks - top[None, :]) * totals, axis=0)
    log_evidence = top + jnp.log(mass)
    share = jnp.exp(peaks - top[None, :]) / mass[None, :]
    numer = jnp.einsum("kp,kpcf->ckf", share, projs, precision=HIGHEST)
    denom = jnp.dot(share * totals, contrast_transfer * contrast_transfer, precision=HIGHEST)
    new_refs = numer / (denom + 1.0)[None]
    return new_refs, log_evidence
```

```python
import math

import jax
import jax.numpy as jnp
from jax import lax
from jax.sharding import PartitionSpec as P

L = 64
BAND = 32
ROT = 8
NRAD = 23
GROUPS = 16


HIGHEST = lax.Precision.HIGHEST


def phase_tables(size, band):
    pixel = jnp.arange(size, dtype=jnp.int32)
    freq = jnp.arange(band, dtype=jnp.int32) - band // 2
    turned = freq[:, None] * pixel[None, :] % size
    angle = turned.astype(jnp.float32) * (2.0 * math.pi / size)
    return (jnp.cos(angle), jnp.sin(angle))


def forward_tables(cosine, sine):
    fcos = cosine / 8.0
    fsin = sine / 8.0
    first_table_part = jnp.stack([fcos.T, -fsin.T], axis=1)
    second_table_part = jnp.stack(
        [jnp.stack([fcos.T, -fsin.T], axis=1), jnp.stack([fsin.T, fcos.T], axis=1)], axis=1
    )
    return (first_table_part, second_table_part)


def inverse_tables(cosine, sine):
    icos = cosine.astype(jnp.bfloat16)
    isin = sine.astype(jnp.bfloat16)
    tab_c = jnp.stack([jnp.stack([icos, isin], axis=1), jnp.stack([-isin, icos], axis=1)], axis=0)
    tab_d = jnp.stack([icos, -isin], axis=0)
    tab_e = jnp.stack([icos.T, isin.T], axis=1)
    tab_f = jnp.stack(
        [jnp.stack([icos.T, isin.T], axis=1), jnp.stack([-isin.T, icos.T], axis=1)], axis=1
    )
    return (tab_c, tab_d, tab_e, tab_f)


def product(form, left, right):
    return jnp.einsum(form, left, right, preferred_element_type=jnp.float32)


def orient(images):
    turned = jnp.swapaxes(images, 1, 2)
    views = [jnp.rot90(images, j, axes=(1, 2)) for j in range(4)]
    views = views + [jnp.rot90(turned, j, axes=(1, 2)) for j in range(4)]
    return jnp.stack(views, axis=1)


def particle_band_rows(images, first_table_part, second_table_part):
    count = images.shape[0]
    oriented = orient(images)
    half = product("nryx,xdb->nrydb", oriented, first_table_part).astype(jnp.bfloat16)
    full = product("nrydb,ydca->nrcab", half, second_table_part).astype(jnp.bfloat16)
    return full.reshape(count, ROT, 2, BAND * BAND)


def class_bands(maps, first_table_part, second_table_part):
    count = maps.shape[0]
    images = maps.reshape(count, L, L)
    half = jnp.einsum("kyx,xdb->kydb", images, first_table_part, precision=HIGHEST)
    full = jnp.einsum("kydb,ydca->kcab", half, second_table_part, precision=HIGHEST)
    return full.reshape(count, 2, BAND * BAND)


def shell_onehot():
    freq = jnp.arange(BAND, dtype=jnp.int32) - BAND // 2
    square = (freq[:, None] ** 2 + freq[None, :] ** 2).reshape(-1)
    bounds = jnp.arange(1, NRAD, dtype=jnp.int32) ** 2
    shell = jnp.sum((square[None, :] >= bounds[:, None]).astype(jnp.int32), axis=0)
    return (shell[None, :] == jnp.arange(NRAD, dtype=jnp.int32)[:, None]).astype(jnp.float32)


def group_onehot(group_ids):
    return (group_ids[:, None] == jnp.arange(GROUPS, dtype=jnp.int32)[None, :]).astype(jnp.float32)


def spectra(ctf_profile, noise_power, group_ids):
    shells = shell_onehot()
    groups = group_onehot(group_ids)
    profile = jnp.dot(groups, ctf_profile, precision=HIGHEST)
    contrast_transfer = jnp.dot(profile, shells, precision=HIGHEST)
    noise_deviation = jnp.dot(noise_power, shells, precision=HIGHEST)
    return (contrast_transfer, noise_deviation)


def class_step(abstract_value, output_value, ref_band, offset, tabs):
    tab_c, tab_d, tab_e, tab_f = tabs
    count = abstract_value.shape[0]
    real_ref = ref_band[0]
    imag_ref = ref_band[1]
    breal = abstract_value[:, :, 0] * real_ref + abstract_value[:, :, 1] * imag_ref
    bimag = abstract_value[:, :, 1] * real_ref - abstract_value[:, :, 0] * imag_ref
    bmat = jnp.stack([breal, bimag], axis=2).astype(jnp.bfloat16).reshape(count, ROT, 2, BAND, BAND)
    edge = product("nrcab,cbdx->nradx", bmat, tab_c).astype(jnp.bfloat16)
    score = product("nradx,day->nyrx", edge, tab_d) - offset[:, None, None, None]
    peak = jnp.max(score, axis=(1, 2, 3))
    expo = jnp.exp(score - peak[:, None, None, None])
    total = jnp.sum(expo, axis=(1, 2, 3))
    uhalf = product("nyrx,xdb->nrydb", expo.astype(jnp.bfloat16), tab_e).astype(jnp.bfloat16)
    what = product("nrydb,ydca->nrcab", uhalf, tab_f).astype(jnp.bfloat16)
    what = what.reshape(count, ROT, 2, BAND * BAND).astype(jnp.float32)
    preal = jnp.sum(
        output_value[:, :, 0] * what[:, :, 0] - output_value[:, :, 1] * what[:, :, 1], axis=1
    )
    pimag = jnp.sum(
        output_value[:, :, 0] * what[:, :, 1] + output_value[:, :, 1] * what[:, :, 0], axis=1
    )
    return (peak, total, jnp.stack([preal, pimag], axis=1))


def shards(particles, group_ids, references, ctf_profile, noise_power):
    cosine, sine = phase_tables(L, BAND)
    first_table_part, second_table_part = forward_tables(cosine, sine)
    tabs = inverse_tables(cosine, sine)
    first_low = first_table_part.astype(jnp.bfloat16)
    second_low = second_table_part.astype(jnp.bfloat16)
    own_bands = particle_band_rows(particles, first_low, second_low)
    count = own_bands.shape[0]
    width = ROT * 2 * BAND * BAND
    label_row = jnp.broadcast_to(group_ids.astype(jnp.bfloat16)[:, None], (count, 128))
    payload = jnp.concatenate([own_bands.reshape(count, width), label_row], axis=1)
    gathered = lax.all_gather(payload, "cls", axis=0, tiled=True)
    fourier_input = gathered[:, :width].reshape(-1, ROT, 2, BAND * BAND)
    block_labels = gathered[:, width].astype(jnp.int32)
    rows = lax.psum(1, "dom")
    spread = jnp.broadcast_to(references[None], (rows,) + references.shape)
    pieces = lax.all_to_all(spread, "dom", 0, 0, tiled=True)
    maps = jnp.transpose(pieces, (1, 0, 2)).reshape(references.shape[0], -1)
    complete_input = fourier_input.astype(jnp.float32)
    contrast_transfer, noise_deviation = spectra(ctf_profile, noise_power, block_labels)
    abstract_value = (
        complete_input * (contrast_transfer / noise_deviation[None, :])[:, None, None, :]
    )
    output_value = complete_input * contrast_transfer[:, None, None, :]
    rbands = class_bands(maps, first_table_part, second_table_part)
    power = rbands[:, 0] ** 2 + rbands[:, 1] ** 2
    offset = 0.5 * jnp.dot(
        contrast_transfer * contrast_transfer / noise_deviation[None, :], power.T, precision=HIGHEST
    )
    peaks, totals, projs = lax.map(
        lambda item: class_step(abstract_value, output_value, item[0], item[1], tabs),
        (rbands, offset.T),
    )
    local_top = jnp.max(peaks, axis=0)
    local_mass = jnp.sum(jnp.exp(peaks - local_top[None, :]) * totals, axis=0)
    summary = lax.all_gather(jnp.stack([local_top, local_mass]), "cls", axis=0)
    top = jnp.max(summary[:, 0], axis=0)
    mass = jnp.sum(jnp.exp(summary[:, 0] - top[None, :]) * summary[:, 1], axis=0)
    log_evidence = top + jnp.log(mass)
    share = jnp.exp(peaks - top[None, :]) / mass[None, :]
    numer = jnp.einsum("kp,kpcf->ckf", share, projs, precision=HIGHEST)
    denom = jnp.dot(share * totals, contrast_transfer * contrast_transfer, precision=HIGHEST)
    stacked = jnp.concatenate([numer, denom[None]], axis=0)
    lanes = stacked.shape[2] // rows
    parts = jnp.moveaxis(stacked.reshape(3, stacked.shape[1], rows, lanes), 2, 0)
    owned = jnp.sum(lax.all_to_all(parts, "dom", 0, 0, tiled=True), axis=0)
    new_refs = owned[:2] / (owned[2] + 1.0)[None]
    return (new_refs, log_evidence)


def solution(mesh):
    in_specs = (P(("dom", "cls"), None, None), P(("dom", "cls")), P("cls", "dom"), P(), P())
    out_specs = (P(None, "cls", "dom"), P("dom"))
    return jax.shard_map(shards, mesh=mesh, in_specs=in_specs, out_specs=out_specs, check_vma=False)
```

```python
import math

import jax
import jax.numpy as jnp
from jax import lax
from jax.sharding import PartitionSpec as P

L = 64
BAND = 32
ROT = 8
NRAD = 23
GROUPS = 16


HIGHEST = lax.Precision.HIGHEST


def phase_tables(size, band):
    pixel = jnp.arange(size, dtype=jnp.int32)
    freq = jnp.arange(band, dtype=jnp.int32) - band // 2
    turned = freq[:, None] * pixel[None, :] % size
    angle = turned.astype(jnp.float32) * (2.0 * math.pi / size)
    return (jnp.cos(angle), jnp.sin(angle))


def forward_tables(cosine, sine):
    fcos = cosine / 8.0
    fsin = sine / 8.0
    first_table_part = jnp.stack([fcos.T, -fsin.T], axis=1)
    second_table_part = jnp.stack(
        [jnp.stack([fcos.T, -fsin.T], axis=1), jnp.stack([fsin.T, fcos.T], axis=1)], axis=1
    )
    return (first_table_part, second_table_part)


def inverse_tables(cosine, sine):
    icos = cosine.astype(jnp.bfloat16)
    isin = sine.astype(jnp.bfloat16)
    tab_c = jnp.stack([jnp.stack([icos, isin], axis=1), jnp.stack([-isin, icos], axis=1)], axis=0)
    tab_d = jnp.stack([icos, -isin], axis=0)
    tab_e = jnp.stack([icos.T, isin.T], axis=1)
    tab_f = jnp.stack(
        [jnp.stack([icos.T, isin.T], axis=1), jnp.stack([-isin.T, icos.T], axis=1)], axis=1
    )
    return (tab_c, tab_d, tab_e, tab_f)


def product(form, left, right):
    return jnp.einsum(form, left, right, preferred_element_type=jnp.float32)


def orient(images):
    turned = jnp.swapaxes(images, 1, 2)
    views = [jnp.rot90(images, j, axes=(1, 2)) for j in range(4)]
    views = views + [jnp.rot90(turned, j, axes=(1, 2)) for j in range(4)]
    return jnp.stack(views, axis=1)


def particle_band_rows(images, first_table_part, second_table_part):
    count = images.shape[0]
    oriented = orient(images)
    half = product("nryx,xdb->nrydb", oriented, first_table_part).astype(jnp.bfloat16)
    full = product("nrydb,ydca->nrcab", half, second_table_part).astype(jnp.bfloat16)
    return full.reshape(count, ROT, 2, BAND * BAND)


def class_bands(maps, first_table_part, second_table_part):
    count = maps.shape[0]
    images = maps.reshape(count, L, L)
    half = jnp.einsum("kyx,xdb->kydb", images, first_table_part, precision=HIGHEST)
    full = jnp.einsum("kydb,ydca->kcab", half, second_table_part, precision=HIGHEST)
    return full.reshape(count, 2, BAND * BAND)


def shell_onehot():
    freq = jnp.arange(BAND, dtype=jnp.int32) - BAND // 2
    square = (freq[:, None] ** 2 + freq[None, :] ** 2).reshape(-1)
    bounds = jnp.arange(1, NRAD, dtype=jnp.int32) ** 2
    shell = jnp.sum((square[None, :] >= bounds[:, None]).astype(jnp.int32), axis=0)
    return (shell[None, :] == jnp.arange(NRAD, dtype=jnp.int32)[:, None]).astype(jnp.float32)


def group_onehot(group_ids):
    return (group_ids[:, None] == jnp.arange(GROUPS, dtype=jnp.int32)[None, :]).astype(jnp.float32)


def spectra(ctf_profile, noise_power, group_ids):
    shells = shell_onehot()
    groups = group_onehot(group_ids)
    profile = jnp.dot(groups, ctf_profile, precision=HIGHEST)
    contrast_transfer = jnp.dot(profile, shells, precision=HIGHEST)
    noise_deviation = jnp.dot(noise_power, shells, precision=HIGHEST)
    return (contrast_transfer, noise_deviation)


def class_step(abstract_value, output_value, ref_bands, offset, tabs):
    tab_c, tab_d, tab_e, tab_f = tabs
    classes = ref_bands.shape[0]
    count = abstract_value.shape[0]
    real_ref = ref_bands[:, None, None, 0]
    imag_ref = ref_bands[:, None, None, 1]
    breal = abstract_value[None, :, :, 0] * real_ref + abstract_value[None, :, :, 1] * imag_ref
    bimag = abstract_value[None, :, :, 1] * real_ref - abstract_value[None, :, :, 0] * imag_ref
    bmat = jnp.stack([breal, bimag], axis=3).astype(jnp.bfloat16)
    bmat = bmat.reshape(classes, count, ROT, 2, BAND, BAND)
    edge = product("knrcab,cbdx->knradx", bmat, tab_c).astype(jnp.bfloat16)
    score = product("knradx,day->knyrx", edge, tab_d) - offset[:, :, None, None, None]
    peak = jnp.max(score, axis=(2, 3, 4))
    expo = jnp.exp(score - peak[:, :, None, None, None])
    total = jnp.sum(expo, axis=(2, 3, 4))
    uhalf = product("knyrx,xdb->knrydb", expo.astype(jnp.bfloat16), tab_e).astype(jnp.bfloat16)
    what = product("knrydb,ydca->knrcab", uhalf, tab_f).astype(jnp.bfloat16)
    what = what.reshape(classes, count, ROT, 2, BAND * BAND).astype(jnp.float32)
    preal = jnp.sum(
        output_value[None, :, :, 0] * what[:, :, :, 0]
        - output_value[None, :, :, 1] * what[:, :, :, 1],
        axis=2,
    )
    pimag = jnp.sum(
        output_value[None, :, :, 0] * what[:, :, :, 1]
        + output_value[None, :, :, 1] * what[:, :, :, 0],
        axis=2,
    )
    return (peak, total, jnp.stack([preal, pimag], axis=2))


def shards(particles, group_ids, references, ctf_profile, noise_power):
    cosine, sine = phase_tables(L, BAND)
    first_table_part, second_table_part = forward_tables(cosine, sine)
    tabs = inverse_tables(cosine, sine)
    first_low = first_table_part.astype(jnp.bfloat16)
    second_low = second_table_part.astype(jnp.bfloat16)
    own_bands = particle_band_rows(particles, first_low, second_low)
    count = own_bands.shape[0]
    width = ROT * 2 * BAND * BAND
    label_row = jnp.broadcast_to(group_ids.astype(jnp.bfloat16)[:, None], (count, 128))
    payload = jnp.concatenate([own_bands.reshape(count, width), label_row], axis=1)
    gathered = lax.all_gather(payload, "cls", axis=0, tiled=True)
    fourier_input = gathered[:, :width].reshape(-1, ROT, 2, BAND * BAND)
    block_labels = gathered[:, width].astype(jnp.int32)
    rows = lax.psum(1, "dom")
    spread = jnp.broadcast_to(references[None], (rows,) + references.shape)
    pieces = lax.all_to_all(spread, "dom", 0, 0, tiled=True)
    maps = jnp.transpose(pieces, (1, 0, 2)).reshape(references.shape[0], -1)
    complete_input = fourier_input.astype(jnp.float32)
    contrast_transfer, noise_deviation = spectra(ctf_profile, noise_power, block_labels)
    abstract_value = (
        complete_input * (contrast_transfer / noise_deviation[None, :])[:, None, None, :]
    )
    output_value = complete_input * contrast_transfer[:, None, None, :]
    rbands = class_bands(maps, first_table_part, second_table_part)
    power = rbands[:, 0] ** 2 + rbands[:, 1] ** 2
    offset = 0.5 * jnp.dot(
        contrast_transfer * contrast_transfer / noise_deviation[None, :], power.T, precision=HIGHEST
    )
    peaks, totals, projs = class_step(abstract_value, output_value, rbands, offset.T, tabs)
    local_top = jnp.max(peaks, axis=0)
    local_mass = jnp.sum(jnp.exp(peaks - local_top[None, :]) * totals, axis=0)
    summary = lax.all_gather(jnp.stack([local_top, local_mass]), "cls", axis=0)
    top = jnp.max(summary[:, 0], axis=0)
    mass = jnp.sum(jnp.exp(summary[:, 0] - top[None, :]) * summary[:, 1], axis=0)
    log_evidence = top + jnp.log(mass)
    share = jnp.exp(peaks - top[None, :]) / mass[None, :]
    numer = jnp.einsum("kp,kpcf->ckf", share, projs, precision=HIGHEST)
    denom = jnp.dot(share * totals, contrast_transfer * contrast_transfer, precision=HIGHEST)
    stacked = jnp.concatenate([numer, denom[None]], axis=0)
    lanes = stacked.shape[2] // rows
    parts = jnp.moveaxis(stacked.reshape(3, stacked.shape[1], rows, lanes), 2, 0)
    owned = jnp.sum(lax.all_to_all(parts, "dom", 0, 0, tiled=True), axis=0)
    new_refs = owned[:2] / (owned[2] + 1.0)[None]
    return (new_refs, log_evidence)


def solution(mesh):
    in_specs = (P(("dom", "cls"), None, None), P(("dom", "cls")), P("cls", "dom"), P(), P())
    out_specs = (P(None, "cls", "dom"), P("dom"))
    return jax.shard_map(shards, mesh=mesh, in_specs=in_specs, out_specs=out_specs, check_vma=False)
```

```python
import math

import jax
import jax.numpy as jnp
from jax import lax
from jax.sharding import PartitionSpec as P

L = 64
BAND = 32
ROT = 8
NRAD = 23
GROUPS = 16


HIGHEST = lax.Precision.HIGHEST


def phase_tables(size, band):
    pixel = jnp.arange(size, dtype=jnp.int32)
    freq = jnp.arange(band, dtype=jnp.int32) - band // 2
    turned = freq[:, None] * pixel[None, :] % size
    angle = turned.astype(jnp.float32) * (2.0 * math.pi / size)
    return (jnp.cos(angle), jnp.sin(angle))


def forward_tables(cosine, sine):
    fcos = cosine / 8.0
    fsin = sine / 8.0
    first_table_part = jnp.stack([fcos.T, -fsin.T], axis=1)
    second_table_part = jnp.stack(
        [jnp.stack([fcos.T, -fsin.T], axis=1), jnp.stack([fsin.T, fcos.T], axis=1)], axis=1
    )
    return (first_table_part, second_table_part)


def inverse_tables(cosine, sine):
    icos = cosine.astype(jnp.bfloat16)
    isin = sine.astype(jnp.bfloat16)
    tab_c = jnp.stack([jnp.stack([icos, isin], axis=1), jnp.stack([-isin, icos], axis=1)], axis=0)
    tab_d = jnp.stack([icos, -isin], axis=0)
    tab_e = jnp.stack([icos.T, isin.T], axis=1)
    tab_f = jnp.stack(
        [jnp.stack([icos.T, isin.T], axis=1), jnp.stack([-isin.T, icos.T], axis=1)], axis=1
    )
    return (tab_c, tab_d, tab_e, tab_f)


def product(form, left, right):
    return jnp.einsum(form, left, right, preferred_element_type=jnp.float32)


def orient(images):
    turned = jnp.swapaxes(images, 1, 2)
    views = [jnp.rot90(images, j, axes=(1, 2)) for j in range(4)]
    views = views + [jnp.rot90(turned, j, axes=(1, 2)) for j in range(4)]
    return jnp.stack(views, axis=1)


def particle_band_rows(images, first_table_part, second_table_part):
    count = images.shape[0]
    oriented = orient(images)
    half = product("nryx,xdb->nrydb", oriented, first_table_part).astype(jnp.bfloat16)
    full = product("nrydb,ydca->nrcab", half, second_table_part).astype(jnp.bfloat16)
    return full.reshape(count, ROT, 2, BAND * BAND)


def class_bands(maps, first_table_part, second_table_part):
    count = maps.shape[0]
    images = maps.reshape(count, L, L)
    half = jnp.einsum("kyx,xdb->kydb", images, first_table_part, precision=HIGHEST)
    full = jnp.einsum("kydb,ydca->kcab", half, second_table_part, precision=HIGHEST)
    return full.reshape(count, 2, BAND * BAND)


def shell_onehot():
    freq = jnp.arange(BAND, dtype=jnp.int32) - BAND // 2
    square = (freq[:, None] ** 2 + freq[None, :] ** 2).reshape(-1)
    bounds = jnp.arange(1, NRAD, dtype=jnp.int32) ** 2
    shell = jnp.sum((square[None, :] >= bounds[:, None]).astype(jnp.int32), axis=0)
    return (shell[None, :] == jnp.arange(NRAD, dtype=jnp.int32)[:, None]).astype(jnp.float32)


def group_onehot(group_ids):
    return (group_ids[:, None] == jnp.arange(GROUPS, dtype=jnp.int32)[None, :]).astype(jnp.float32)


def spectra(ctf_profile, noise_power, group_ids):
    shells = shell_onehot()
    groups = group_onehot(group_ids)
    profile = jnp.dot(groups, ctf_profile, precision=HIGHEST)
    contrast_transfer = jnp.dot(profile, shells, precision=HIGHEST)
    noise_deviation = jnp.dot(noise_power, shells, precision=HIGHEST)
    return (contrast_transfer, noise_deviation)


def class_step(abstract_value, output_value, ref_bands, offset, tabs):
    tab_c, tab_d, tab_e, tab_f = tabs
    classes = ref_bands.shape[0]
    count = abstract_value.shape[0]
    real_ref = ref_bands[:, None, None, 0]
    imag_ref = ref_bands[:, None, None, 1]
    breal = abstract_value[None, :, :, 0] * real_ref + abstract_value[None, :, :, 1] * imag_ref
    bimag = abstract_value[None, :, :, 1] * real_ref - abstract_value[None, :, :, 0] * imag_ref
    bmat = jnp.stack([breal, bimag], axis=3).astype(jnp.bfloat16)
    bmat = bmat.reshape(classes, count, ROT, 2, BAND, BAND)
    edge = product("knrcab,cbdx->knradx", bmat, tab_c).astype(jnp.bfloat16)
    score = product("knradx,day->knyrx", edge, tab_d) - offset[:, :, None, None, None]
    peak = jnp.max(score, axis=(2, 3, 4))
    expo = jnp.exp(score - peak[:, :, None, None, None])
    total = jnp.sum(expo, axis=(2, 3, 4))
    uhalf = product("knyrx,xdb->knrydb", expo.astype(jnp.bfloat16), tab_e).astype(jnp.bfloat16)
    what = product("knrydb,ydca->knrcab", uhalf, tab_f).astype(jnp.bfloat16)
    what = what.astype(jnp.float32)
    yval = output_value.reshape(count, ROT, 2, BAND, BAND)
    preal = jnp.sum(
        yval[None, :, :, 0] * what[:, :, :, 0] - yval[None, :, :, 1] * what[:, :, :, 1],
        axis=2,
    )
    pimag = jnp.sum(
        yval[None, :, :, 0] * what[:, :, :, 1] + yval[None, :, :, 1] * what[:, :, :, 0],
        axis=2,
    )
    proj = jnp.stack([preal, pimag], axis=2)
    return (peak, total, proj.reshape(classes, count, 2, BAND * BAND))


def shards(particles, group_ids, references, ctf_profile, noise_power):
    cosine, sine = phase_tables(L, BAND)
    first_table_part, second_table_part = forward_tables(cosine, sine)
    tabs = inverse_tables(cosine, sine)
    first_low = first_table_part.astype(jnp.bfloat16)
    second_low = second_table_part.astype(jnp.bfloat16)
    own_bands = particle_band_rows(particles, first_low, second_low)
    count = own_bands.shape[0]
    width = ROT * 2 * BAND * BAND
    label_row = jnp.broadcast_to(group_ids.astype(jnp.bfloat16)[:, None], (count, 128))
    payload = jnp.concatenate([own_bands.reshape(count, width), label_row], axis=1)
    peers = lax.psum(1, "cls")
    gathered = lax.all_to_all(
        jnp.broadcast_to(payload, (peers,) + payload.shape[1:]), "cls", 0, 0, tiled=True
    )
    fourier_input = gathered[:, :width].reshape(-1, ROT, 2, BAND * BAND)
    block_labels = gathered[:, width].astype(jnp.int32)
    rows = lax.psum(1, "dom")
    spread = jnp.broadcast_to(references[None], (rows,) + references.shape)
    pieces = lax.all_to_all(spread, "dom", 0, 0, tiled=True)
    maps = jnp.transpose(pieces, (1, 0, 2)).reshape(references.shape[0], -1)
    complete_input = fourier_input.astype(jnp.float32)
    contrast_transfer, noise_deviation = spectra(ctf_profile, noise_power, block_labels)
    abstract_value = (
        complete_input * (contrast_transfer / noise_deviation[None, :])[:, None, None, :]
    )
    output_value = complete_input * contrast_transfer[:, None, None, :]
    rbands = class_bands(maps, first_table_part, second_table_part)
    power = rbands[:, 0] ** 2 + rbands[:, 1] ** 2
    offset = 0.5 * jnp.dot(
        contrast_transfer * contrast_transfer / noise_deviation[None, :], power.T, precision=HIGHEST
    )
    peaks, totals, projs = class_step(abstract_value, output_value, rbands, offset.T, tabs)
    local_top = jnp.max(peaks, axis=0)
    local_mass = jnp.sum(jnp.exp(peaks - local_top[None, :]) * totals, axis=0)
    own_summary = jnp.stack([local_top, local_mass])
    summary = lax.all_to_all(
        jnp.broadcast_to(own_summary[None], (peers,) + own_summary.shape), "cls", 0, 0, tiled=True
    )
    top = jnp.max(summary[:, 0], axis=0)
    mass = jnp.sum(jnp.exp(summary[:, 0] - top[None, :]) * summary[:, 1], axis=0)
    log_evidence = top + jnp.log(mass)
    share = jnp.exp(peaks - top[None, :]) / mass[None, :]
    numer = jnp.einsum("kp,kpcf->ckf", share, projs, precision=HIGHEST)
    denom = jnp.dot(share * totals, contrast_transfer * contrast_transfer, precision=HIGHEST)
    stacked = jnp.concatenate([numer, denom[None]], axis=0)
    lanes = stacked.shape[2] // rows
    parts = jnp.moveaxis(stacked.reshape(3, stacked.shape[1], rows, lanes), 2, 0)
    owned = jnp.sum(lax.all_to_all(parts, "dom", 0, 0, tiled=True), axis=0)
    new_refs = owned[:2] / (owned[2] + 1.0)[None]
    return (new_refs, log_evidence)


def solution(mesh):
    in_specs = (P(("dom", "cls"), None, None), P(("dom", "cls")), P("cls", "dom"), P(), P())
    out_specs = (P(None, "cls", "dom"), P("dom"))
    return jax.shard_map(shards, mesh=mesh, in_specs=in_specs, out_specs=out_specs, check_vma=False)
```

```python
import math

import jax
import jax.numpy as jnp
from jax import lax
from jax.sharding import PartitionSpec as P

L = 64
BAND = 32
ROT = 8
NRAD = 23
GROUPS = 16


HIGHEST = lax.Precision.HIGHEST


def phase_tables(size, band):
    pixel = jnp.arange(size, dtype=jnp.int32)
    freq = jnp.arange(band, dtype=jnp.int32) - band // 2
    turned = freq[:, None] * pixel[None, :] % size
    angle = turned.astype(jnp.float32) * (2.0 * math.pi / size)
    return (jnp.cos(angle), jnp.sin(angle))


def forward_tables(cosine, sine):
    fcos = cosine / 8.0
    fsin = sine / 8.0
    first_table_part = jnp.stack([fcos.T, -fsin.T], axis=1)
    second_table_part = jnp.stack(
        [jnp.stack([fcos.T, -fsin.T], axis=1), jnp.stack([fsin.T, fcos.T], axis=1)], axis=1
    )
    return (first_table_part, second_table_part)


def inverse_tables(cosine, sine):
    icos = cosine.astype(jnp.bfloat16)
    isin = sine.astype(jnp.bfloat16)
    tab_c = jnp.stack([jnp.stack([icos, isin], axis=1), jnp.stack([-isin, icos], axis=1)], axis=0)
    tab_d = jnp.stack([icos, -isin], axis=0)
    tab_e = jnp.stack([icos.T, isin.T], axis=1)
    tab_f = jnp.stack(
        [jnp.stack([icos.T, isin.T], axis=1), jnp.stack([-isin.T, icos.T], axis=1)], axis=1
    )
    return (tab_c, tab_d, tab_e, tab_f)


def product(form, left, right):
    return jnp.einsum(form, left, right, preferred_element_type=jnp.float32)


def orient(images):
    turned = jnp.swapaxes(images, 1, 2)
    views = [jnp.rot90(images, j, axes=(1, 2)) for j in range(4)]
    views = views + [jnp.rot90(turned, j, axes=(1, 2)) for j in range(4)]
    return jnp.stack(views, axis=1)


def particle_band_rows(images, first_table_part, second_table_part):
    count = images.shape[0]
    oriented = orient(images)
    half = product("nryx,xdb->nrydb", oriented, first_table_part).astype(jnp.bfloat16)
    full = product("nrydb,ydca->nrcab", half, second_table_part).astype(jnp.bfloat16)
    return full.reshape(count, ROT, 2, BAND * BAND)


def class_bands(maps, first_table_part, second_table_part):
    count = maps.shape[0]
    images = maps.reshape(count, L, L)
    half = jnp.einsum("kyx,xdb->kydb", images, first_table_part, precision=HIGHEST)
    full = jnp.einsum("kydb,ydca->kcab", half, second_table_part, precision=HIGHEST)
    return full.reshape(count, 2, BAND * BAND)


def shell_onehot():
    freq = jnp.arange(BAND, dtype=jnp.int32) - BAND // 2
    square = (freq[:, None] ** 2 + freq[None, :] ** 2).reshape(-1)
    bounds = jnp.arange(1, NRAD, dtype=jnp.int32) ** 2
    shell = jnp.sum((square[None, :] >= bounds[:, None]).astype(jnp.int32), axis=0)
    return (shell[None, :] == jnp.arange(NRAD, dtype=jnp.int32)[:, None]).astype(jnp.float32)


def group_onehot(group_ids):
    return (group_ids[:, None] == jnp.arange(GROUPS, dtype=jnp.int32)[None, :]).astype(jnp.float32)


def spectra(ctf_profile, noise_power, group_ids):
    shells = shell_onehot()
    groups = group_onehot(group_ids)
    profile = jnp.dot(groups, ctf_profile, precision=HIGHEST)
    contrast_transfer = jnp.dot(profile, shells, precision=HIGHEST)
    noise_deviation = jnp.dot(noise_power, shells, precision=HIGHEST)
    return (contrast_transfer, noise_deviation)


def class_step(abstract_value, output_value, ref_bands, offset, tabs):
    tab_c, tab_d, tab_e, tab_f = tabs
    classes = ref_bands.shape[0]
    count = abstract_value.shape[0]
    real_ref = ref_bands[:, None, None, 0]
    imag_ref = ref_bands[:, None, None, 1]
    breal = abstract_value[None, :, :, 0] * real_ref + abstract_value[None, :, :, 1] * imag_ref
    bimag = abstract_value[None, :, :, 1] * real_ref - abstract_value[None, :, :, 0] * imag_ref
    lead = (classes, count, ROT)
    bmat = jnp.stack(
        [breal.reshape(lead + (BAND, BAND)), bimag.reshape(lead + (BAND, BAND))], axis=4
    ).astype(jnp.bfloat16)
    edge = product("mk,kn->mn", bmat.reshape(-1, 2 * BAND), tab_c.reshape(2 * BAND, 2 * L))
    edge = edge.astype(jnp.bfloat16).reshape(lead + (BAND, 2, L))
    edge = jnp.transpose(edge, (0, 1, 2, 5, 4, 3)).reshape(-1, 2 * BAND)
    score = product("mk,kn->mn", edge, tab_d.reshape(2 * BAND, L))
    score = score.reshape(classes, count, ROT * L, L) - offset[:, :, None, None]
    peak = jnp.max(score, axis=(2, 3))
    expo = jnp.exp(score - peak[:, :, None, None])
    total = jnp.sum(expo, axis=(2, 3))
    expo_low = jnp.transpose(expo.astype(jnp.bfloat16).reshape(lead + (L, L)), (0, 1, 2, 4, 3))
    uhalf = product("mk,kn->mn", expo_low.reshape(-1, L), tab_e.reshape(L, 2 * BAND))
    uhalf = uhalf.astype(jnp.bfloat16).reshape(lead + (L, 2, BAND))
    uhalf = jnp.transpose(uhalf, (0, 1, 2, 5, 3, 4)).reshape(-1, 2 * L)
    what = product("mk,kn->mn", uhalf, tab_f.reshape(2 * L, 2 * BAND)).astype(jnp.bfloat16)
    what = what.astype(jnp.float32).reshape(lead + (BAND, 2, BAND))
    yval = jnp.transpose(output_value.reshape(count, ROT, 2, BAND, BAND), (0, 1, 4, 2, 3))
    preal = jnp.sum(
        yval[None, :, :, :, 0] * what[:, :, :, :, 0] - yval[None, :, :, :, 1] * what[:, :, :, :, 1],
        axis=2,
    )
    pimag = jnp.sum(
        yval[None, :, :, :, 0] * what[:, :, :, :, 1] + yval[None, :, :, :, 1] * what[:, :, :, :, 0],
        axis=2,
    )
    proj = jnp.transpose(jnp.stack([preal, pimag], axis=2), (0, 1, 2, 4, 3))
    return (peak, total, proj.reshape(classes, count, 2, BAND * BAND))


def shards(particles, group_ids, references, ctf_profile, noise_power):
    cosine, sine = phase_tables(L, BAND)
    first_table_part, second_table_part = forward_tables(cosine, sine)
    tabs = inverse_tables(cosine, sine)
    first_low = first_table_part.astype(jnp.bfloat16)
    second_low = second_table_part.astype(jnp.bfloat16)
    own_bands = particle_band_rows(particles, first_low, second_low)
    count = own_bands.shape[0]
    width = ROT * 2 * BAND * BAND
    label_row = jnp.broadcast_to(group_ids.astype(jnp.bfloat16)[:, None], (count, 128))
    payload = jnp.concatenate([own_bands.reshape(count, width), label_row], axis=1)
    peers = lax.psum(1, "cls")
    gathered = lax.all_to_all(
        jnp.broadcast_to(payload, (peers,) + payload.shape[1:]), "cls", 0, 0, tiled=True
    )
    fourier_input = gathered[:, :width].reshape(-1, ROT, 2, BAND * BAND)
    block_labels = gathered[:, width].astype(jnp.int32)
    rows = lax.psum(1, "dom")
    spread = jnp.broadcast_to(references[None], (rows,) + references.shape)
    pieces = lax.all_to_all(spread, "dom", 0, 0, tiled=True)
    maps = jnp.transpose(pieces, (1, 0, 2)).reshape(references.shape[0], -1)
    complete_input = fourier_input.astype(jnp.float32)
    contrast_transfer, noise_deviation = spectra(ctf_profile, noise_power, block_labels)
    abstract_value = (
        complete_input * (contrast_transfer / noise_deviation[None, :])[:, None, None, :]
    )
    output_value = complete_input * contrast_transfer[:, None, None, :]
    rbands = class_bands(maps, first_table_part, second_table_part)
    power = rbands[:, 0] ** 2 + rbands[:, 1] ** 2
    offset = 0.5 * jnp.dot(
        contrast_transfer * contrast_transfer / noise_deviation[None, :], power.T, precision=HIGHEST
    )
    peaks, totals, projs = class_step(abstract_value, output_value, rbands, offset.T, tabs)
    local_top = jnp.max(peaks, axis=0)
    local_mass = jnp.sum(jnp.exp(peaks - local_top[None, :]) * totals, axis=0)
    own_summary = jnp.stack([local_top, local_mass])
    summary = lax.all_to_all(
        jnp.broadcast_to(own_summary[None], (peers,) + own_summary.shape), "cls", 0, 0, tiled=True
    )
    top = jnp.max(summary[:, 0], axis=0)
    mass = jnp.sum(jnp.exp(summary[:, 0] - top[None, :]) * summary[:, 1], axis=0)
    log_evidence = top + jnp.log(mass)
    share = jnp.exp(peaks - top[None, :]) / mass[None, :]
    numer = jnp.einsum("kp,kpcf->ckf", share, projs, precision=HIGHEST)
    denom = jnp.dot(share * totals, contrast_transfer * contrast_transfer, precision=HIGHEST)
    stacked = jnp.concatenate([numer, denom[None]], axis=0)
    lanes = stacked.shape[2] // rows
    parts = jnp.moveaxis(stacked.reshape(3, stacked.shape[1], rows, lanes), 2, 0)
    owned = jnp.sum(lax.all_to_all(parts, "dom", 0, 0, tiled=True), axis=0)
    new_refs = owned[:2] / (owned[2] + 1.0)[None]
    return (new_refs, log_evidence)


def solution(mesh):
    in_specs = (P(("dom", "cls"), None, None), P(("dom", "cls")), P("cls", "dom"), P(), P())
    out_specs = (P(None, "cls", "dom"), P("dom"))
    return jax.shard_map(shards, mesh=mesh, in_specs=in_specs, out_specs=out_specs, check_vma=False)
```

```python
import math

import jax
import jax.numpy as jnp
from jax import lax
from jax.sharding import PartitionSpec as P

L = 64
BAND = 32
ROT = 8
NRAD = 23
GROUPS = 16


HIGHEST = lax.Precision.HIGHEST


def phase_tables(size, band):
    pixel = jnp.arange(size, dtype=jnp.int32)
    freq = jnp.arange(band, dtype=jnp.int32) - band // 2
    turned = freq[:, None] * pixel[None, :] % size
    angle = turned.astype(jnp.float32) * (2.0 * math.pi / size)
    return (jnp.cos(angle), jnp.sin(angle))


def forward_tables(cosine, sine):
    fcos = cosine / 8.0
    fsin = sine / 8.0
    first_table_part = jnp.stack([fcos.T, -fsin.T], axis=1)
    second_table_part = jnp.stack(
        [jnp.stack([fcos.T, -fsin.T], axis=1), jnp.stack([fsin.T, fcos.T], axis=1)], axis=1
    )
    return (first_table_part, second_table_part)


def inverse_tables(cosine, sine):
    icos = cosine.astype(jnp.bfloat16)
    isin = sine.astype(jnp.bfloat16)
    tab_c = jnp.stack([jnp.stack([icos, isin], axis=1), jnp.stack([-isin, icos], axis=1)], axis=0)
    tab_d = jnp.stack([icos, -isin], axis=0)
    tab_e = jnp.stack([icos.T, isin.T], axis=1)
    tab_f = jnp.stack(
        [jnp.stack([icos.T, isin.T], axis=1), jnp.stack([-isin.T, icos.T], axis=1)], axis=1
    )
    return (tab_c, tab_d, tab_e, tab_f)


def product(form, left, right):
    return jnp.einsum(form, left, right, preferred_element_type=jnp.float32)


def orient(images):
    turned = jnp.swapaxes(images, 1, 2)
    views = [jnp.rot90(images, j, axes=(1, 2)) for j in range(4)]
    views = views + [jnp.rot90(turned, j, axes=(1, 2)) for j in range(4)]
    return jnp.stack(views, axis=1)


def particle_band_rows(images, first_table_part, second_table_part):
    count = images.shape[0]
    oriented = orient(images)
    half = product("nryx,xdb->nrydb", oriented, first_table_part).astype(jnp.bfloat16)
    full = product("nrydb,ydca->nrcab", half, second_table_part).astype(jnp.bfloat16)
    return full.reshape(count, ROT, 2, BAND * BAND)


def class_bands(maps, first_table_part, second_table_part):
    count = maps.shape[0]
    images = maps.reshape(count, L, L)
    half = jnp.einsum("kyx,xdb->kydb", images, first_table_part, precision=HIGHEST)
    full = jnp.einsum("kydb,ydca->kcab", half, second_table_part, precision=HIGHEST)
    return full.reshape(count, 2, BAND * BAND)


def shell_onehot():
    freq = jnp.arange(BAND, dtype=jnp.int32) - BAND // 2
    square = (freq[:, None] ** 2 + freq[None, :] ** 2).reshape(-1)
    bounds = jnp.arange(1, NRAD, dtype=jnp.int32) ** 2
    shell = jnp.sum((square[None, :] >= bounds[:, None]).astype(jnp.int32), axis=0)
    return (shell[None, :] == jnp.arange(NRAD, dtype=jnp.int32)[:, None]).astype(jnp.float32)


def group_onehot(group_ids):
    return (group_ids[:, None] == jnp.arange(GROUPS, dtype=jnp.int32)[None, :]).astype(jnp.float32)


def spectra(ctf_profile, noise_power, group_ids):
    shells = shell_onehot()
    groups = group_onehot(group_ids)
    profile = jnp.dot(groups, ctf_profile, precision=HIGHEST)
    contrast_transfer = jnp.dot(profile, shells, precision=HIGHEST)
    noise_deviation = jnp.dot(noise_power, shells, precision=HIGHEST)
    return (contrast_transfer, noise_deviation)


def class_step(abstract_value, output_value, ref_bands, offset, tabs):
    tab_c, tab_d, tab_e, tab_f = tabs
    classes = ref_bands.shape[0]
    count = abstract_value.shape[0]
    real_ref = ref_bands[:, None, None, 0]
    imag_ref = ref_bands[:, None, None, 1]
    breal = abstract_value[None, :, :, 0] * real_ref + abstract_value[None, :, :, 1] * imag_ref
    bimag = abstract_value[None, :, :, 1] * real_ref - abstract_value[None, :, :, 0] * imag_ref
    bmat = jnp.stack([breal, bimag], axis=3).astype(jnp.bfloat16)
    bmat = bmat.reshape(classes, count, ROT, 2, BAND, BAND)
    edge = product("knrcab,cbdx->knradx", bmat, tab_c).astype(jnp.bfloat16)
    score = product("knradx,day->knyrx", edge, tab_d) - offset[:, :, None, None, None]
    peak = jnp.max(score, axis=(2, 3, 4))
    expo = jnp.exp(score - peak[:, :, None, None, None])
    total = jnp.sum(expo, axis=(2, 3, 4))
    uhalf = product("knyrx,xdb->knrydb", expo.astype(jnp.bfloat16), tab_e).astype(jnp.bfloat16)
    what = product("knrydb,ydca->knrcab", uhalf, tab_f).astype(jnp.bfloat16)
    what = what.astype(jnp.float32)
    yval = output_value.reshape(count, ROT, 2, BAND, BAND)
    preal = jnp.sum(
        yval[None, :, :, 0] * what[:, :, :, 0] - yval[None, :, :, 1] * what[:, :, :, 1],
        axis=2,
    )
    pimag = jnp.sum(
        yval[None, :, :, 0] * what[:, :, :, 1] + yval[None, :, :, 1] * what[:, :, :, 0],
        axis=2,
    )
    proj = jnp.stack([preal, pimag], axis=2)
    return (peak, total, proj.reshape(classes, count, 2, BAND * BAND))


def shards(particles, group_ids, references, ctf_profile, noise_power):
    cosine, sine = phase_tables(L, BAND)
    first_table_part, second_table_part = forward_tables(cosine, sine)
    tabs = inverse_tables(cosine, sine)
    first_low = first_table_part.astype(jnp.bfloat16)
    second_low = second_table_part.astype(jnp.bfloat16)
    own_bands = particle_band_rows(particles, first_low, second_low)
    count = own_bands.shape[0]
    width = ROT * 2 * BAND * BAND
    label_row = jnp.broadcast_to(group_ids.astype(jnp.bfloat16)[:, None], (count, 128))
    payload = jnp.concatenate([own_bands.reshape(count, width), label_row], axis=1)
    peers = lax.psum(1, "cls")
    gathered = lax.all_to_all(
        jnp.broadcast_to(payload, (peers,) + payload.shape[1:]), "cls", 0, 0, tiled=True
    )
    fourier_input = gathered[:, :width].reshape(-1, ROT, 2, BAND * BAND)
    block_labels = gathered[:, width].astype(jnp.int32)
    rows = lax.psum(1, "dom")
    spread = jnp.broadcast_to(references[None], (rows,) + references.shape)
    pieces = lax.all_to_all(spread, "dom", 0, 0, tiled=True)
    maps = jnp.transpose(pieces, (1, 0, 2)).reshape(references.shape[0], -1)
    complete_input = fourier_input.astype(jnp.float32)
    contrast_transfer, noise_deviation = spectra(ctf_profile, noise_power, block_labels)
    abstract_value = (
        complete_input * (contrast_transfer / noise_deviation[None, :])[:, None, None, :]
    )
    output_value = complete_input * contrast_transfer[:, None, None, :]
    rbands = class_bands(maps, first_table_part, second_table_part)
    power = rbands[:, 0] ** 2 + rbands[:, 1] ** 2
    offset = 0.5 * jnp.dot(
        contrast_transfer * contrast_transfer / noise_deviation[None, :], power.T, precision=HIGHEST
    )
    peaks, totals, projs = class_step(abstract_value, output_value, rbands, offset.T, tabs)
    peaks, totals = lax.optimization_barrier((peaks, totals))
    local_top = jnp.max(peaks, axis=0)
    local_mass = jnp.sum(jnp.exp(peaks - local_top[None, :]) * totals, axis=0)
    own_summary = jnp.stack([local_top, local_mass])
    summary = lax.all_to_all(
        jnp.broadcast_to(own_summary[None], (peers,) + own_summary.shape), "cls", 0, 0, tiled=True
    )
    top = jnp.max(summary[:, 0], axis=0)
    mass = jnp.sum(jnp.exp(summary[:, 0] - top[None, :]) * summary[:, 1], axis=0)
    log_evidence = top + jnp.log(mass)
    share = jnp.exp(peaks - top[None, :]) / mass[None, :]
    numer = jnp.einsum("kp,kpcf->ckf", share, projs, precision=HIGHEST)
    denom = jnp.dot(share * totals, contrast_transfer * contrast_transfer, precision=HIGHEST)
    stacked = jnp.concatenate([numer, denom[None]], axis=0)
    lanes = stacked.shape[2] // rows
    parts = jnp.moveaxis(stacked.reshape(3, stacked.shape[1], rows, lanes), 2, 0)
    owned = jnp.sum(lax.all_to_all(parts, "dom", 0, 0, tiled=True), axis=0)
    new_refs = owned[:2] / (owned[2] + 1.0)[None]
    return (new_refs, log_evidence)


def solution(mesh):
    in_specs = (P(("dom", "cls"), None, None), P(("dom", "cls")), P("cls", "dom"), P(), P())
    out_specs = (P(None, "cls", "dom"), P("dom"))
    return jax.shard_map(shards, mesh=mesh, in_specs=in_specs, out_specs=out_specs, check_vma=False)
```

```python
import math

import jax
import jax.numpy as jnp
from jax import lax
from jax.sharding import PartitionSpec as P

L = 64
BAND = 32
ROT = 8
NRAD = 23
GROUPS = 16


HIGHEST = lax.Precision.HIGHEST


def phase_tables(size, band):
    pixel = jnp.arange(size, dtype=jnp.int32)
    freq = jnp.arange(band, dtype=jnp.int32) - band // 2
    turned = freq[:, None] * pixel[None, :] % size
    angle = turned.astype(jnp.float32) * (2.0 * math.pi / size)
    return (jnp.cos(angle), jnp.sin(angle))


def forward_tables(cosine, sine):
    fcos = cosine / 8.0
    fsin = sine / 8.0
    first_table_part = jnp.stack([fcos.T, -fsin.T], axis=1)
    second_table_part = jnp.stack(
        [jnp.stack([fcos.T, -fsin.T], axis=1), jnp.stack([fsin.T, fcos.T], axis=1)], axis=1
    )
    return (first_table_part, second_table_part)


def inverse_tables(cosine, sine):
    icos = cosine.astype(jnp.bfloat16)
    isin = sine.astype(jnp.bfloat16)
    tab_c = jnp.stack([jnp.stack([icos, isin], axis=1), jnp.stack([-isin, icos], axis=1)], axis=0)
    tab_d = jnp.stack([icos, -isin], axis=0)
    tab_e = jnp.stack([icos.T, isin.T], axis=1)
    tab_f = jnp.stack(
        [jnp.stack([icos.T, isin.T], axis=1), jnp.stack([-isin.T, icos.T], axis=1)], axis=1
    )
    return (tab_c, tab_d, tab_e, tab_f)


def product(form, left, right):
    return jnp.einsum(form, left, right, preferred_element_type=jnp.float32)


def orient(images):
    turned = jnp.swapaxes(images, 1, 2)
    views = [jnp.rot90(images, j, axes=(1, 2)) for j in range(4)]
    views = views + [jnp.rot90(turned, j, axes=(1, 2)) for j in range(4)]
    return jnp.stack(views, axis=1)


def particle_band_rows(images, first_table_part, second_table_part):
    count = images.shape[0]
    oriented = orient(images)
    half = product("nryx,xdb->nrydb", oriented, first_table_part).astype(jnp.bfloat16)
    full = product("nrydb,ydca->nrcab", half, second_table_part).astype(jnp.bfloat16)
    return full.reshape(count, ROT, 2, BAND * BAND)


def class_bands(maps, first_table_part, second_table_part):
    count = maps.shape[0]
    images = maps.reshape(count, L, L)
    half = jnp.einsum("kyx,xdb->kydb", images, first_table_part, precision=HIGHEST)
    full = jnp.einsum("kydb,ydca->kcab", half, second_table_part, precision=HIGHEST)
    return full.reshape(count, 2, BAND * BAND)


def shell_onehot():
    freq = jnp.arange(BAND, dtype=jnp.int32) - BAND // 2
    square = (freq[:, None] ** 2 + freq[None, :] ** 2).reshape(-1)
    bounds = jnp.arange(1, NRAD, dtype=jnp.int32) ** 2
    shell = jnp.sum((square[None, :] >= bounds[:, None]).astype(jnp.int32), axis=0)
    return (shell[None, :] == jnp.arange(NRAD, dtype=jnp.int32)[:, None]).astype(jnp.float32)


def group_onehot(group_ids):
    return (group_ids[:, None] == jnp.arange(GROUPS, dtype=jnp.int32)[None, :]).astype(jnp.float32)


def spectra(ctf_profile, noise_power, group_ids):
    shells = shell_onehot()
    groups = group_onehot(group_ids)
    profile = jnp.dot(groups, ctf_profile, precision=HIGHEST)
    contrast_transfer = jnp.dot(profile, shells, precision=HIGHEST)
    noise_deviation = jnp.dot(noise_power, shells, precision=HIGHEST)
    return (contrast_transfer, noise_deviation)


def class_step(abstract_value, output_value, ref_bands, offset, tabs):
    tab_c, tab_d, tab_e, tab_f = tabs
    classes = ref_bands.shape[0]
    count = abstract_value.shape[0]
    real_ref = ref_bands[:, None, None, 0]
    imag_ref = ref_bands[:, None, None, 1]
    breal = abstract_value[None, :, :, 0] * real_ref + abstract_value[None, :, :, 1] * imag_ref
    bimag = abstract_value[None, :, :, 1] * real_ref - abstract_value[None, :, :, 0] * imag_ref
    bmat = jnp.stack([breal, bimag], axis=3).astype(jnp.bfloat16)
    bmat = bmat.reshape(classes, count, ROT, 2, BAND, BAND)
    edge = product("knrcab,cbdx->knradx", bmat, tab_c).astype(jnp.bfloat16)
    score = product("knradx,day->knyrx", edge, tab_d) - offset[:, :, None, None, None]
    peak = jnp.max(score, axis=(2, 3, 4))
    expo = jnp.exp(score - peak[:, :, None, None, None])
    total = jnp.sum(expo, axis=(2, 3, 4))
    expo_low, total = lax.optimization_barrier((expo.astype(jnp.bfloat16), total))
    uhalf = product("knyrx,xdb->knrydb", expo_low, tab_e).astype(jnp.bfloat16)
    what = product("knrydb,ydca->knrcab", uhalf, tab_f).astype(jnp.bfloat16)
    what = what.astype(jnp.float32)
    yval = output_value.reshape(count, ROT, 2, BAND, BAND)
    preal = jnp.sum(
        yval[None, :, :, 0] * what[:, :, :, 0] - yval[None, :, :, 1] * what[:, :, :, 1],
        axis=2,
    )
    pimag = jnp.sum(
        yval[None, :, :, 0] * what[:, :, :, 1] + yval[None, :, :, 1] * what[:, :, :, 0],
        axis=2,
    )
    proj = jnp.stack([preal, pimag], axis=2)
    return (peak, total, proj.reshape(classes, count, 2, BAND * BAND))


def shards(particles, group_ids, references, ctf_profile, noise_power):
    cosine, sine = phase_tables(L, BAND)
    first_table_part, second_table_part = forward_tables(cosine, sine)
    tabs = inverse_tables(cosine, sine)
    first_low = first_table_part.astype(jnp.bfloat16)
    second_low = second_table_part.astype(jnp.bfloat16)
    own_bands = particle_band_rows(particles, first_low, second_low)
    count = own_bands.shape[0]
    width = ROT * 2 * BAND * BAND
    label_row = jnp.broadcast_to(group_ids.astype(jnp.bfloat16)[:, None], (count, 128))
    payload = jnp.concatenate([own_bands.reshape(count, width), label_row], axis=1)
    peers = lax.psum(1, CLS)
    gathered = lax.all_to_all(
        jnp.broadcast_to(payload, (peers,) + payload.shape[1:]), CLS, 0, 0, tiled=True
    )
    fourier_input = gathered[:, :width].reshape(-1, ROT, 2, BAND * BAND)
    block_labels = gathered[:, width].astype(jnp.int32)
    rows = lax.psum(1, DOM)
    width_y = lax.psum(1, "y")
    width_z = lax.psum(1, "z_hi")
    width_c = lax.psum(1, "core")
    first = lax.all_to_all(
        jnp.broadcast_to(references[None], (width_y,) + references.shape), "y", 0, 0, tiled=True
    )
    second = lax.all_to_all(
        jnp.broadcast_to(first[None], (width_z * width_c,) + first.shape),
        ("z_hi", "core"),
        0,
        0,
        tiled=True,
    )
    pieces = second.reshape((width_z, width_c, width_y) + references.shape)
    pieces = jnp.transpose(pieces, (3, 0, 2, 1, 4)).reshape(references.shape[0], -1)
    maps = pieces
    complete_input = fourier_input.astype(jnp.float32)
    contrast_transfer, noise_deviation = spectra(ctf_profile, noise_power, block_labels)
    abstract_value = (
        complete_input * (contrast_transfer / noise_deviation[None, :])[:, None, None, :]
    )
    output_value = complete_input * contrast_transfer[:, None, None, :]
    rbands = class_bands(maps, first_table_part, second_table_part)
    power = rbands[:, 0] ** 2 + rbands[:, 1] ** 2
    offset = 0.5 * jnp.dot(
        contrast_transfer * contrast_transfer / noise_deviation[None, :], power.T, precision=HIGHEST
    )
    peaks, totals, projs = class_step(abstract_value, output_value, rbands, offset.T, tabs)
    peaks, totals = lax.optimization_barrier((peaks, totals))
    local_top = jnp.max(peaks, axis=0)
    local_mass = jnp.sum(jnp.exp(peaks - local_top[None, :]) * totals, axis=0)
    own_summary = jnp.stack([local_top, local_mass])
    summary = lax.all_to_all(
        jnp.broadcast_to(own_summary[None], (peers,) + own_summary.shape), CLS, 0, 0, tiled=True
    )
    top = jnp.max(summary[:, 0], axis=0)
    mass = jnp.sum(jnp.exp(summary[:, 0] - top[None, :]) * summary[:, 1], axis=0)
    log_evidence = top + jnp.log(mass)
    share = jnp.exp(peaks - top[None, :]) / mass[None, :]
    numer = jnp.einsum("kp,kpcf->ckf", share, projs, precision=HIGHEST)
    denom = jnp.dot(share * totals, contrast_transfer * contrast_transfer, precision=HIGHEST)
    stacked = jnp.concatenate([numer, denom[None]], axis=0)
    lanes = stacked.shape[2] // rows
    split = stacked.reshape(3, stacked.shape[1], width_z, width_y, width_c, lanes)
    step = jnp.sum(lax.all_to_all(jnp.moveaxis(split, 3, 0), "y", 0, 0, tiled=True), axis=0)
    step = jnp.transpose(step, (2, 3, 0, 1, 4)).reshape(width_z * width_c, 3, -1, lanes)
    owned = jnp.sum(lax.all_to_all(step, ("z_hi", "core"), 0, 0, tiled=True), axis=0)
    new_refs = owned[:2] / (owned[2] + 1.0)[None]
    return (new_refs, log_evidence)


DOM = ("z_hi", "y", "core")
CLS = ("z_lo", "x")


def solution(mesh):
    dom, cls = mesh.devices.shape
    fine = jax.sharding.Mesh(mesh.devices.reshape(4, dom // 8, 2, 2, cls // 2), DOM + CLS)
    in_specs = (P(DOM + CLS, None, None), P(DOM + CLS), P(CLS, DOM), P(), P())
    out_specs = (P(None, CLS, DOM), P(DOM))
    return jax.shard_map(shards, mesh=fine, in_specs=in_specs, out_specs=out_specs, check_vma=False)
```

```python
import math

import jax
import jax.numpy as jnp
from jax import lax
from jax.sharding import PartitionSpec as P

L = 64
BAND = 32
ROT = 8
NRAD = 23
GROUPS = 16


HIGHEST = lax.Precision.HIGHEST


def phase_tables(size, band):
    pixel = jnp.arange(size, dtype=jnp.int32)
    freq = jnp.arange(band, dtype=jnp.int32) - band // 2
    turned = freq[:, None] * pixel[None, :] % size
    angle = turned.astype(jnp.float32) * (2.0 * math.pi / size)
    return (jnp.cos(angle), jnp.sin(angle))


def forward_tables(cosine, sine):
    fcos = cosine / 8.0
    fsin = sine / 8.0
    first_table_part = jnp.stack([fcos.T, -fsin.T], axis=1)
    second_table_part = jnp.stack(
        [jnp.stack([fcos.T, -fsin.T], axis=1), jnp.stack([fsin.T, fcos.T], axis=1)], axis=1
    )
    return (first_table_part, second_table_part)


def inverse_tables(cosine, sine):
    icos = cosine.astype(jnp.bfloat16)
    isin = sine.astype(jnp.bfloat16)
    tab_c = jnp.stack([jnp.stack([icos, isin], axis=1), jnp.stack([-isin, icos], axis=1)], axis=0)
    tab_d = jnp.stack([icos, -isin], axis=0)
    tab_e = jnp.stack([icos.T, isin.T], axis=1)
    tab_f = jnp.stack(
        [jnp.stack([icos.T, isin.T], axis=1), jnp.stack([-isin.T, icos.T], axis=1)], axis=1
    )
    return (tab_c, tab_d, tab_e, tab_f)


def product(form, left, right):
    return jnp.einsum(form, left, right, preferred_element_type=jnp.float32)


def orient(images):
    turned = jnp.swapaxes(images, 1, 2)
    views = [jnp.rot90(images, j, axes=(1, 2)) for j in range(4)]
    views = views + [jnp.rot90(turned, j, axes=(1, 2)) for j in range(4)]
    return jnp.stack(views, axis=1)


def particle_band_rows(images, first_table_part, second_table_part):
    count = images.shape[0]
    oriented = orient(images)
    half = product("nryx,xdb->nrydb", oriented, first_table_part).astype(jnp.bfloat16)
    full = product("nrydb,ydca->nrcab", half, second_table_part).astype(jnp.bfloat16)
    return full.reshape(count, ROT, 2, BAND * BAND)


def class_bands(maps, first_table_part, second_table_part):
    count = maps.shape[0]
    images = maps.reshape(count, L, L)
    half = jnp.einsum("kyx,xdb->kydb", images, first_table_part, precision=HIGHEST)
    full = jnp.einsum("kydb,ydca->kcab", half, second_table_part, precision=HIGHEST)
    return full.reshape(count, 2, BAND * BAND)


def shell_onehot():
    freq = jnp.arange(BAND, dtype=jnp.int32) - BAND // 2
    square = (freq[:, None] ** 2 + freq[None, :] ** 2).reshape(-1)
    bounds = jnp.arange(1, NRAD, dtype=jnp.int32) ** 2
    shell = jnp.sum((square[None, :] >= bounds[:, None]).astype(jnp.int32), axis=0)
    return (shell[None, :] == jnp.arange(NRAD, dtype=jnp.int32)[:, None]).astype(jnp.float32)


def group_onehot(group_ids):
    return (group_ids[:, None] == jnp.arange(GROUPS, dtype=jnp.int32)[None, :]).astype(jnp.float32)


def spectra(ctf_profile, noise_power, group_ids):
    shells = shell_onehot()
    groups = group_onehot(group_ids)
    profile = jnp.dot(groups, ctf_profile, precision=HIGHEST)
    contrast_transfer = jnp.dot(profile, shells, precision=HIGHEST)
    noise_deviation = jnp.dot(noise_power, shells, precision=HIGHEST)
    return (contrast_transfer, noise_deviation)


def merge_scaled(left, right):
    left_top, left_sum = left
    right_top, right_sum = right
    top = jnp.maximum(left_top, right_top)
    left_scale = jnp.where(left_top == top, 1.0, jnp.exp(left_top - top))
    right_scale = jnp.where(right_top == top, 1.0, jnp.exp(right_top - top))
    return (top, left_sum * left_scale + right_sum * right_scale)


def class_step(abstract_value, output_value, ref_bands, offset, tabs):
    tab_c, tab_d, tab_e, tab_f = tabs
    classes = ref_bands.shape[0]
    count = abstract_value.shape[0]
    real_ref = ref_bands[:, None, None, 0]
    imag_ref = ref_bands[:, None, None, 1]
    breal = abstract_value[None, :, :, 0] * real_ref + abstract_value[None, :, :, 1] * imag_ref
    bimag = abstract_value[None, :, :, 1] * real_ref - abstract_value[None, :, :, 0] * imag_ref
    bmat = jnp.stack([breal, bimag], axis=3).astype(jnp.bfloat16)
    bmat = bmat.reshape(classes, count, ROT, 2, BAND, BAND)
    edge = product("knrcab,cbdx->knradx", bmat, tab_c).astype(jnp.bfloat16)
    score = product("knradx,day->knyrx", edge, tab_d) - offset[:, :, None, None, None]
    peak, total = lax.reduce(
        (score, jnp.ones_like(score)),
        (jnp.array(-jnp.inf, score.dtype), jnp.array(0.0, score.dtype)),
        merge_scaled,
        (2, 3, 4),
    )
    expo = jnp.exp(score - peak[:, :, None, None, None])
    uhalf = product("knyrx,xdb->knrydb", expo.astype(jnp.bfloat16), tab_e).astype(jnp.bfloat16)
    what = product("knrydb,ydca->knrcab", uhalf, tab_f).astype(jnp.bfloat16)
    what = what.astype(jnp.float32)
    yval = output_value.reshape(count, ROT, 2, BAND, BAND)
    preal = jnp.sum(
        yval[None, :, :, 0] * what[:, :, :, 0] - yval[None, :, :, 1] * what[:, :, :, 1],
        axis=2,
    )
    pimag = jnp.sum(
        yval[None, :, :, 0] * what[:, :, :, 1] + yval[None, :, :, 1] * what[:, :, :, 0],
        axis=2,
    )
    proj = jnp.stack([preal, pimag], axis=2)
    return (peak, total, proj.reshape(classes, count, 2, BAND * BAND))


def shards(particles, group_ids, references, ctf_profile, noise_power):
    cosine, sine = phase_tables(L, BAND)
    first_table_part, second_table_part = forward_tables(cosine, sine)
    tabs = inverse_tables(cosine, sine)
    first_low = first_table_part.astype(jnp.bfloat16)
    second_low = second_table_part.astype(jnp.bfloat16)
    own_bands = particle_band_rows(particles, first_low, second_low)
    count = own_bands.shape[0]
    width = ROT * 2 * BAND * BAND
    label_row = jnp.broadcast_to(group_ids.astype(jnp.bfloat16)[:, None], (count, 128))
    payload = jnp.concatenate([own_bands.reshape(count, width), label_row], axis=1)
    peers = lax.psum(1, "cls")
    gathered = lax.all_to_all(
        jnp.broadcast_to(payload, (peers,) + payload.shape[1:]), "cls", 0, 0, tiled=True
    )
    fourier_input = gathered[:, :width].reshape(-1, ROT, 2, BAND * BAND)
    block_labels = gathered[:, width].astype(jnp.int32)
    rows = lax.psum(1, "dom")
    spread = jnp.broadcast_to(references[None], (rows,) + references.shape)
    pieces = lax.all_to_all(spread, "dom", 0, 0, tiled=True)
    maps = jnp.transpose(pieces, (1, 0, 2)).reshape(references.shape[0], -1)
    complete_input = fourier_input.astype(jnp.float32)
    contrast_transfer, noise_deviation = spectra(ctf_profile, noise_power, block_labels)
    abstract_value = (
        complete_input * (contrast_transfer / noise_deviation[None, :])[:, None, None, :]
    )
    output_value = complete_input * contrast_transfer[:, None, None, :]
    rbands = class_bands(maps, first_table_part, second_table_part)
    power = rbands[:, 0] ** 2 + rbands[:, 1] ** 2
    offset = 0.5 * jnp.dot(
        contrast_transfer * contrast_transfer / noise_deviation[None, :], power.T, precision=HIGHEST
    )
    peaks, totals, projs = class_step(abstract_value, output_value, rbands, offset.T, tabs)
    peaks, totals = lax.optimization_barrier((peaks, totals))
    local_top = jnp.max(peaks, axis=0)
    local_mass = jnp.sum(jnp.exp(peaks - local_top[None, :]) * totals, axis=0)
    own_summary = jnp.stack([local_top, local_mass])
    summary = lax.all_to_all(
        jnp.broadcast_to(own_summary[None], (peers,) + own_summary.shape), "cls", 0, 0, tiled=True
    )
    top = jnp.max(summary[:, 0], axis=0)
    mass = jnp.sum(jnp.exp(summary[:, 0] - top[None, :]) * summary[:, 1], axis=0)
    log_evidence = top + jnp.log(mass)
    share = jnp.exp(peaks - top[None, :]) / mass[None, :]
    numer = jnp.einsum("kp,kpcf->ckf", share, projs, precision=HIGHEST)
    denom = jnp.dot(share * totals, contrast_transfer * contrast_transfer, precision=HIGHEST)
    stacked = jnp.concatenate([numer, denom[None]], axis=0)
    lanes = stacked.shape[2] // rows
    parts = jnp.moveaxis(stacked.reshape(3, stacked.shape[1], rows, lanes), 2, 0)
    owned = jnp.sum(lax.all_to_all(parts, "dom", 0, 0, tiled=True), axis=0)
    new_refs = owned[:2] / (owned[2] + 1.0)[None]
    return (new_refs, log_evidence)


def solution(mesh):
    in_specs = (P(("dom", "cls"), None, None), P(("dom", "cls")), P("cls", "dom"), P(), P())
    out_specs = (P(None, "cls", "dom"), P("dom"))
    return jax.shard_map(shards, mesh=mesh, in_specs=in_specs, out_specs=out_specs, check_vma=False)
```

```python
import math

import jax
import jax.numpy as jnp
from jax import lax
from jax.sharding import PartitionSpec as P

L = 64
BAND = 32
ROT = 8
NRAD = 23
GROUPS = 16


HIGHEST = lax.Precision.HIGHEST


def phase_tables(size, band):
    pixel = jnp.arange(size, dtype=jnp.int32)
    freq = jnp.arange(band, dtype=jnp.int32) - band // 2
    turned = freq[:, None] * pixel[None, :] % size
    angle = turned.astype(jnp.float32) * (2.0 * math.pi / size)
    return (jnp.cos(angle), jnp.sin(angle))


def forward_tables(cosine, sine):
    fcos = cosine / 8.0
    fsin = sine / 8.0
    first_table_part = jnp.stack([fcos.T, -fsin.T], axis=1)
    second_table_part = jnp.stack(
        [jnp.stack([fcos.T, -fsin.T], axis=1), jnp.stack([fsin.T, fcos.T], axis=1)], axis=1
    )
    return (first_table_part, second_table_part)


def inverse_tables(cosine, sine):
    icos = cosine.astype(jnp.bfloat16)
    isin = sine.astype(jnp.bfloat16)
    tab_c = jnp.stack([jnp.stack([icos, isin], axis=1), jnp.stack([-isin, icos], axis=1)], axis=0)
    tab_d = jnp.stack([icos, -isin], axis=0)
    tab_e = jnp.stack([icos.T, isin.T], axis=1)
    tab_f = jnp.stack(
        [jnp.stack([icos.T, isin.T], axis=1), jnp.stack([-isin.T, icos.T], axis=1)], axis=1
    )
    return (tab_c, tab_d, tab_e, tab_f)


def product(form, left, right):
    return jnp.einsum(form, left, right, preferred_element_type=jnp.float32)


def orient(images):
    turned = jnp.swapaxes(images, 1, 2)
    views = [jnp.rot90(images, j, axes=(1, 2)) for j in range(4)]
    views = views + [jnp.rot90(turned, j, axes=(1, 2)) for j in range(4)]
    return jnp.stack(views, axis=1)


def particle_band_rows(images, first_table_part, second_table_part):
    count = images.shape[0]
    oriented = orient(images)
    half = product("nryx,xdb->nrydb", oriented, first_table_part).astype(jnp.bfloat16)
    full = product("nrydb,ydca->nrcab", half, second_table_part).astype(jnp.bfloat16)
    return full.reshape(count, ROT, 2, BAND * BAND)


def class_bands(maps, first_table_part, second_table_part):
    count = maps.shape[0]
    images = maps.reshape(count, L, L)
    half = jnp.einsum("kyx,xdb->kydb", images, first_table_part, precision=HIGHEST)
    full = jnp.einsum("kydb,ydca->kcab", half, second_table_part, precision=HIGHEST)
    return full.reshape(count, 2, BAND * BAND)


def shell_onehot():
    freq = jnp.arange(BAND, dtype=jnp.int32) - BAND // 2
    square = (freq[:, None] ** 2 + freq[None, :] ** 2).reshape(-1)
    bounds = jnp.arange(1, NRAD, dtype=jnp.int32) ** 2
    shell = jnp.sum((square[None, :] >= bounds[:, None]).astype(jnp.int32), axis=0)
    return (shell[None, :] == jnp.arange(NRAD, dtype=jnp.int32)[:, None]).astype(jnp.float32)


def group_onehot(group_ids):
    return (group_ids[:, None] == jnp.arange(GROUPS, dtype=jnp.int32)[None, :]).astype(jnp.float32)


def spectra(ctf_profile, noise_power, group_ids):
    shells = shell_onehot()
    groups = group_onehot(group_ids)
    profile = jnp.dot(groups, ctf_profile, precision=HIGHEST)
    contrast_transfer = jnp.dot(profile, shells, precision=HIGHEST)
    noise_deviation = jnp.dot(noise_power, shells, precision=HIGHEST)
    return (contrast_transfer, noise_deviation)


def class_step(abstract_value, output_value, ref_bands, offset, tabs):
    tab_c, tab_d, tab_e, tab_f = tabs
    classes = ref_bands.shape[0]
    count = abstract_value.shape[0]
    real_ref = ref_bands[:, None, None, 0]
    imag_ref = ref_bands[:, None, None, 1]
    breal = abstract_value[None, :, :, 0] * real_ref + abstract_value[None, :, :, 1] * imag_ref
    bimag = abstract_value[None, :, :, 1] * real_ref - abstract_value[None, :, :, 0] * imag_ref
    bmat = jnp.stack([breal, bimag], axis=3).astype(jnp.bfloat16)
    bmat = bmat.reshape(classes, count, ROT, 2, BAND, BAND)
    edge = product("knrcab,cbdx->knradx", bmat, tab_c).astype(jnp.bfloat16)
    score = product("knradx,day->knyrx", edge, tab_d) - offset[:, :, None, None, None]
    peak = jnp.max(score, axis=(2, 3, 4))
    expo = jnp.exp(score - peak[:, :, None, None, None])
    total = jnp.sum(expo, axis=(2, 3, 4))
    uhalf = product("knyrx,xdb->knrydb", expo.astype(jnp.bfloat16), tab_e).astype(jnp.bfloat16)
    what = product("knrydb,ydca->knrcab", uhalf, tab_f).astype(jnp.bfloat16)
    what = what.astype(jnp.float32)
    yval = output_value.reshape(count, ROT, 2, BAND, BAND)
    preal = jnp.sum(
        yval[None, :, :, 0] * what[:, :, :, 0] - yval[None, :, :, 1] * what[:, :, :, 1],
        axis=2,
    )
    pimag = jnp.sum(
        yval[None, :, :, 0] * what[:, :, :, 1] + yval[None, :, :, 1] * what[:, :, :, 0],
        axis=2,
    )
    proj = jnp.stack([preal, pimag], axis=2)
    return (peak, total, proj.reshape(classes, count, 2, BAND * BAND))


def shards(particles, group_ids, references, ctf_profile, noise_power):
    cosine, sine = phase_tables(L, BAND)
    first_table_part, second_table_part = forward_tables(cosine, sine)
    tabs = inverse_tables(cosine, sine)
    first_low = first_table_part.astype(jnp.bfloat16)
    second_low = second_table_part.astype(jnp.bfloat16)
    count = particles.shape[0]
    width = L * L
    label_row = jnp.broadcast_to(group_ids.astype(jnp.bfloat16)[:, None], (count, 128))
    payload = jnp.concatenate([particles.reshape(count, width), label_row], axis=1)
    peers = lax.psum(1, "cls")
    gathered = lax.all_to_all(
        jnp.broadcast_to(payload, (peers,) + payload.shape[1:]), "cls", 0, 0, tiled=True
    )
    images = gathered[:, :width].reshape(-1, L, L)
    fourier_input = particle_band_rows(images, first_low, second_low)
    block_labels = gathered[:, width].astype(jnp.int32)
    rows = lax.psum(1, "dom")
    spread = jnp.broadcast_to(references[None], (rows,) + references.shape)
    pieces = lax.all_to_all(spread, "dom", 0, 0, tiled=True)
    maps = jnp.transpose(pieces, (1, 0, 2)).reshape(references.shape[0], -1)
    complete_input = fourier_input.astype(jnp.float32)
    contrast_transfer, noise_deviation = spectra(ctf_profile, noise_power, block_labels)
    abstract_value = (
        complete_input * (contrast_transfer / noise_deviation[None, :])[:, None, None, :]
    )
    output_value = complete_input * contrast_transfer[:, None, None, :]
    rbands = class_bands(maps, first_table_part, second_table_part)
    power = rbands[:, 0] ** 2 + rbands[:, 1] ** 2
    offset = 0.5 * jnp.dot(
        contrast_transfer * contrast_transfer / noise_deviation[None, :], power.T, precision=HIGHEST
    )
    peaks, totals, projs = class_step(abstract_value, output_value, rbands, offset.T, tabs)
    peaks, totals = lax.optimization_barrier((peaks, totals))
    local_top = jnp.max(peaks, axis=0)
    local_mass = jnp.sum(jnp.exp(peaks - local_top[None, :]) * totals, axis=0)
    own_summary = jnp.stack([local_top, local_mass])
    summary = lax.all_to_all(
        jnp.broadcast_to(own_summary[None], (peers,) + own_summary.shape), "cls", 0, 0, tiled=True
    )
    top = jnp.max(summary[:, 0], axis=0)
    mass = jnp.sum(jnp.exp(summary[:, 0] - top[None, :]) * summary[:, 1], axis=0)
    log_evidence = top + jnp.log(mass)
    share = jnp.exp(peaks - top[None, :]) / mass[None, :]
    numer = jnp.einsum("kp,kpcf->ckf", share, projs, precision=HIGHEST)
    denom = jnp.dot(share * totals, contrast_transfer * contrast_transfer, precision=HIGHEST)
    stacked = jnp.concatenate([numer, denom[None]], axis=0)
    lanes = stacked.shape[2] // rows
    parts = jnp.moveaxis(stacked.reshape(3, stacked.shape[1], rows, lanes), 2, 0)
    owned = jnp.sum(lax.all_to_all(parts, "dom", 0, 0, tiled=True), axis=0)
    new_refs = owned[:2] / (owned[2] + 1.0)[None]
    return (new_refs, log_evidence)


def solution(mesh):
    in_specs = (P(("dom", "cls"), None, None), P(("dom", "cls")), P("cls", "dom"), P(), P())
    out_specs = (P(None, "cls", "dom"), P("dom"))
    return jax.shard_map(shards, mesh=mesh, in_specs=in_specs, out_specs=out_specs, check_vma=False)
```

```python
import math

import jax
import jax.numpy as jnp
from jax import lax
from jax.sharding import PartitionSpec as P

L = 64
BAND = 32
ROT = 8
NRAD = 23
GROUPS = 16


HIGHEST = lax.Precision.HIGHEST


def phase_tables(size, band):
    pixel = jnp.arange(size, dtype=jnp.int32)
    freq = jnp.arange(band, dtype=jnp.int32) - band // 2
    turned = freq[:, None] * pixel[None, :] % size
    angle = turned.astype(jnp.float32) * (2.0 * math.pi / size)
    return (jnp.cos(angle), jnp.sin(angle))


def forward_tables(cosine, sine):
    fcos = cosine / 8.0
    fsin = sine / 8.0
    first_table_part = jnp.stack([fcos.T, -fsin.T], axis=1)
    second_table_part = jnp.stack(
        [jnp.stack([fcos.T, -fsin.T], axis=1), jnp.stack([fsin.T, fcos.T], axis=1)], axis=1
    )
    return (first_table_part, second_table_part)


def inverse_tables(cosine, sine):
    icos = cosine.astype(jnp.bfloat16)
    isin = sine.astype(jnp.bfloat16)
    tab_c = jnp.stack([jnp.stack([icos, isin], axis=1), jnp.stack([-isin, icos], axis=1)], axis=0)
    tab_d = jnp.stack([icos, -isin], axis=0)
    tab_e = jnp.stack([icos.T, isin.T], axis=1)
    tab_f = jnp.stack(
        [jnp.stack([icos.T, isin.T], axis=1), jnp.stack([-isin.T, icos.T], axis=1)], axis=1
    )
    return (tab_c, tab_d, tab_e, tab_f)


def product(form, left, right):
    return jnp.einsum(form, left, right, preferred_element_type=jnp.float32)


def orient(images):
    turned = jnp.swapaxes(images, 1, 2)
    views = [jnp.rot90(images, j, axes=(1, 2)) for j in range(4)]
    views = views + [jnp.rot90(turned, j, axes=(1, 2)) for j in range(4)]
    return jnp.stack(views, axis=1)


def particle_band_rows(images, first_table_part, second_table_part):
    count = images.shape[0]
    oriented = orient(images)
    half = product("nryx,xdb->nrydb", oriented, first_table_part).astype(jnp.bfloat16)
    full = product("nrydb,ydca->nrcab", half, second_table_part).astype(jnp.bfloat16)
    return full.reshape(count, ROT, 2, BAND * BAND)


def class_bands(maps, first_table_part, second_table_part):
    count = maps.shape[0]
    images = maps.reshape(count, L, L)
    half = jnp.einsum("kyx,xdb->kydb", images, first_table_part, precision=HIGHEST)
    full = jnp.einsum("kydb,ydca->kcab", half, second_table_part, precision=HIGHEST)
    return full.reshape(count, 2, BAND * BAND)


def shell_onehot():
    freq = jnp.arange(BAND, dtype=jnp.int32) - BAND // 2
    square = (freq[:, None] ** 2 + freq[None, :] ** 2).reshape(-1)
    bounds = jnp.arange(1, NRAD, dtype=jnp.int32) ** 2
    shell = jnp.sum((square[None, :] >= bounds[:, None]).astype(jnp.int32), axis=0)
    return (shell[None, :] == jnp.arange(NRAD, dtype=jnp.int32)[:, None]).astype(jnp.float32)


def group_onehot(group_ids):
    return (group_ids[:, None] == jnp.arange(GROUPS, dtype=jnp.int32)[None, :]).astype(jnp.float32)


def spectra(ctf_profile, noise_power, group_ids):
    shells = shell_onehot()
    groups = group_onehot(group_ids)
    profile = jnp.dot(groups, ctf_profile, precision=HIGHEST)
    contrast_transfer = jnp.dot(profile, shells, precision=HIGHEST)
    noise_deviation = jnp.dot(noise_power, shells, precision=HIGHEST)
    return (contrast_transfer, noise_deviation)


def class_step(abstract_value, output_value, ref_bands, offset, tabs):
    tab_c, tab_d, tab_e, tab_f = tabs
    classes = ref_bands.shape[0]
    count = abstract_value.shape[0]
    real_ref = ref_bands[:, None, None, 0]
    imag_ref = ref_bands[:, None, None, 1]
    breal = abstract_value[None, :, :, 0] * real_ref + abstract_value[None, :, :, 1] * imag_ref
    bimag = abstract_value[None, :, :, 1] * real_ref - abstract_value[None, :, :, 0] * imag_ref
    bmat = jnp.stack([breal, bimag], axis=3).astype(jnp.bfloat16)
    bmat = bmat.reshape(classes, count, ROT, 2, BAND, BAND)
    edge = product("knrcab,cbdx->knradx", bmat, tab_c).astype(jnp.bfloat16)
    score = product("knradx,day->knyrx", edge, tab_d) - offset[:, :, None, None, None]
    peak = jnp.max(score, axis=(2, 3, 4))
    expo = jnp.exp(score - peak[:, :, None, None, None])
    total = jnp.sum(expo, axis=(2, 3, 4))
    uhalf = product("knyrx,xdb->knrydb", expo.astype(jnp.bfloat16), tab_e).astype(jnp.bfloat16)
    what = product("knrydb,ydca->knrcab", uhalf, tab_f).astype(jnp.bfloat16)
    what = what.astype(jnp.float32)
    yval = output_value.reshape(count, ROT, 2, BAND, BAND)
    preal = jnp.sum(
        yval[None, :, :, 0] * what[:, :, :, 0] - yval[None, :, :, 1] * what[:, :, :, 1],
        axis=2,
    )
    pimag = jnp.sum(
        yval[None, :, :, 0] * what[:, :, :, 1] + yval[None, :, :, 1] * what[:, :, :, 0],
        axis=2,
    )
    proj = jnp.stack([preal, pimag], axis=2)
    return (peak, total, proj.reshape(classes, count, 2, BAND * BAND))


def shards(particles, group_ids, references, ctf_profile, noise_power):
    cosine, sine = phase_tables(L, BAND)
    first_table_part, second_table_part = forward_tables(cosine, sine)
    tabs = inverse_tables(cosine, sine)
    first_low = first_table_part.astype(jnp.bfloat16)
    second_low = second_table_part.astype(jnp.bfloat16)
    count = particles.shape[0]
    width = L * L
    label_row = jnp.broadcast_to(group_ids.astype(jnp.bfloat16)[:, None], (count, 128))
    payload = jnp.concatenate([particles.reshape(count, width), label_row], axis=1)
    peers = lax.psum(1, "cls")
    gathered = lax.all_to_all(
        jnp.broadcast_to(payload, (peers,) + payload.shape[1:]), "cls", 0, 0, tiled=True
    )
    images = gathered[:, :width].reshape(-1, L, L)
    fourier_input = particle_band_rows(images, first_low, second_low)
    block_labels = gathered[:, width].astype(jnp.int32)
    rows = lax.psum(1, "dom")
    spread = jnp.broadcast_to(references[None], (rows,) + references.shape)
    pieces = lax.all_to_all(spread, "dom", 0, 0, tiled=True)
    maps = jnp.transpose(pieces, (1, 0, 2)).reshape(references.shape[0], -1)
    complete_input = lax.reduce_precision(fourier_input.astype(jnp.float32), 8, 7)
    contrast_transfer, noise_deviation = spectra(ctf_profile, noise_power, block_labels)
    abstract_value = (
        complete_input * (contrast_transfer / noise_deviation[None, :])[:, None, None, :]
    )
    output_value = complete_input * contrast_transfer[:, None, None, :]
    rbands = class_bands(maps, first_table_part, second_table_part)
    power = rbands[:, 0] ** 2 + rbands[:, 1] ** 2
    offset = 0.5 * jnp.dot(
        contrast_transfer * contrast_transfer / noise_deviation[None, :], power.T, precision=HIGHEST
    )
    peaks, totals, projs = class_step(abstract_value, output_value, rbands, offset.T, tabs)
    peaks, totals = lax.optimization_barrier((peaks, totals))
    local_top = jnp.max(peaks, axis=0)
    local_mass = jnp.sum(jnp.exp(peaks - local_top[None, :]) * totals, axis=0)
    own_summary = jnp.stack([local_top, local_mass])
    summary = lax.all_to_all(
        jnp.broadcast_to(own_summary[None], (peers,) + own_summary.shape), "cls", 0, 0, tiled=True
    )
    top = jnp.max(summary[:, 0], axis=0)
    mass = jnp.sum(jnp.exp(summary[:, 0] - top[None, :]) * summary[:, 1], axis=0)
    log_evidence = top + jnp.log(mass)
    share = jnp.exp(peaks - top[None, :]) / mass[None, :]
    numer = jnp.einsum("kp,kpcf->ckf", share, projs, precision=HIGHEST)
    denom = jnp.dot(share * totals, contrast_transfer * contrast_transfer, precision=HIGHEST)
    stacked = jnp.concatenate([numer, denom[None]], axis=0)
    lanes = stacked.shape[2] // rows
    parts = jnp.moveaxis(stacked.reshape(3, stacked.shape[1], rows, lanes), 2, 0)
    owned = jnp.sum(lax.all_to_all(parts, "dom", 0, 0, tiled=True), axis=0)
    new_refs = owned[:2] / (owned[2] + 1.0)[None]
    return (new_refs, log_evidence)


def solution(mesh):
    in_specs = (P(("dom", "cls"), None, None), P(("dom", "cls")), P("cls", "dom"), P(), P())
    out_specs = (P(None, "cls", "dom"), P("dom"))
    return jax.shard_map(shards, mesh=mesh, in_specs=in_specs, out_specs=out_specs, check_vma=False)
```

```python
import math

import jax
import jax.numpy as jnp
from jax import lax
from jax.sharding import PartitionSpec as P

L = 64
BAND = 32
ROT = 8
NRAD = 23
GROUPS = 16


HIGHEST = lax.Precision.HIGHEST


def phase_tables(size, band):
    pixel = jnp.arange(size, dtype=jnp.int32)
    freq = jnp.arange(band, dtype=jnp.int32) - band // 2
    turned = freq[:, None] * pixel[None, :] % size
    angle = turned.astype(jnp.float32) * (2.0 * math.pi / size)
    return (jnp.cos(angle), jnp.sin(angle))


def forward_tables(cosine, sine):
    fcos = cosine / 8.0
    fsin = sine / 8.0
    first_table_part = jnp.stack([fcos.T, -fsin.T], axis=1)
    second_table_part = jnp.stack(
        [jnp.stack([fcos.T, -fsin.T], axis=1), jnp.stack([fsin.T, fcos.T], axis=1)], axis=1
    )
    return (first_table_part, second_table_part)


def inverse_tables(cosine, sine):
    icos = cosine.astype(jnp.bfloat16)
    isin = sine.astype(jnp.bfloat16)
    tab_c = jnp.stack([jnp.stack([icos, isin], axis=1), jnp.stack([-isin, icos], axis=1)], axis=0)
    tab_d = jnp.stack([icos, -isin], axis=0)
    tab_e = jnp.stack([icos.T, isin.T], axis=1)
    tab_f = jnp.stack(
        [jnp.stack([icos.T, isin.T], axis=1), jnp.stack([-isin.T, icos.T], axis=1)], axis=1
    )
    return (tab_c, tab_d, tab_e, tab_f)


def product(form, left, right):
    return jnp.einsum(form, left, right, preferred_element_type=jnp.float32)


def orient(images):
    turned = jnp.swapaxes(images, 1, 2)
    views = [jnp.rot90(images, j, axes=(1, 2)) for j in range(4)]
    views = views + [jnp.rot90(turned, j, axes=(1, 2)) for j in range(4)]
    return jnp.stack(views, axis=1)


def particle_band_rows(images, first_table_part, second_table_part):
    count = images.shape[0]
    oriented = orient(images)
    half = product("nryx,xdb->nrydb", oriented, first_table_part).astype(jnp.bfloat16)
    full = product("nrydb,ydca->nrcab", half, second_table_part).astype(jnp.bfloat16)
    return full.reshape(count, ROT, 2, BAND * BAND)


def class_bands(maps, first_table_part, second_table_part):
    count = maps.shape[0]
    images = maps.reshape(count, L, L)
    half = jnp.einsum("kyx,xdb->kydb", images, first_table_part, precision=HIGHEST)
    full = jnp.einsum("kydb,ydca->kcab", half, second_table_part, precision=HIGHEST)
    return full.reshape(count, 2, BAND * BAND)


def shell_onehot():
    freq = jnp.arange(BAND, dtype=jnp.int32) - BAND // 2
    square = (freq[:, None] ** 2 + freq[None, :] ** 2).reshape(-1)
    bounds = jnp.arange(1, NRAD, dtype=jnp.int32) ** 2
    shell = jnp.sum((square[None, :] >= bounds[:, None]).astype(jnp.int32), axis=0)
    return (shell[None, :] == jnp.arange(NRAD, dtype=jnp.int32)[:, None]).astype(jnp.float32)


def group_onehot(group_ids):
    return (group_ids[:, None] == jnp.arange(GROUPS, dtype=jnp.int32)[None, :]).astype(jnp.float32)


def spectra(ctf_profile, noise_power, group_ids):
    shells = shell_onehot()
    groups = group_onehot(group_ids)
    profile = jnp.dot(groups, ctf_profile, precision=HIGHEST)
    contrast_transfer = jnp.dot(profile, shells, precision=HIGHEST)
    noise_deviation = jnp.dot(noise_power, shells, precision=HIGHEST)
    return (contrast_transfer, noise_deviation)


def class_step(abstract_value, output_value, ref_bands, offset, tabs):
    tab_c, tab_d, tab_e, tab_f = tabs
    classes = ref_bands.shape[0]
    count = abstract_value.shape[0]
    real_ref = ref_bands[:, None, None, 0]
    imag_ref = ref_bands[:, None, None, 1]
    breal = abstract_value[None, :, :, 0] * real_ref + abstract_value[None, :, :, 1] * imag_ref
    bimag = abstract_value[None, :, :, 1] * real_ref - abstract_value[None, :, :, 0] * imag_ref
    bmat = jnp.stack([breal, bimag], axis=3).astype(jnp.bfloat16)
    bmat = bmat.reshape(classes, count, ROT, 2, BAND, BAND)
    edge = product("knrcab,cbdx->knradx", bmat, tab_c).astype(jnp.bfloat16)
    score = product("knradx,day->knyrx", edge, tab_d) - offset[:, :, None, None, None]
    peak = jnp.max(score, axis=(2, 3, 4))
    expo = jnp.exp(score - peak[:, :, None, None, None])
    total = jnp.sum(expo, axis=(2, 3, 4))
    uhalf = product("knyrx,xdb->knrydb", expo.astype(jnp.bfloat16), tab_e).astype(jnp.bfloat16)
    what = product("knrydb,ydca->knrcab", uhalf, tab_f).astype(jnp.bfloat16)
    what = what.astype(jnp.float32)
    yval = output_value.reshape(count, ROT, 2, BAND, BAND)
    preal = jnp.sum(
        yval[None, :, :, 0] * what[:, :, :, 0] - yval[None, :, :, 1] * what[:, :, :, 1],
        axis=2,
    )
    pimag = jnp.sum(
        yval[None, :, :, 0] * what[:, :, :, 1] + yval[None, :, :, 1] * what[:, :, :, 0],
        axis=2,
    )
    proj = jnp.stack([preal, pimag], axis=2)
    return (peak, total, proj.reshape(classes, count, 2, BAND * BAND))


def shards(particles, group_ids, references, ctf_profile, noise_power):
    cosine, sine = phase_tables(L, BAND)
    first_table_part, second_table_part = forward_tables(cosine, sine)
    tabs = inverse_tables(cosine, sine)
    first_low = first_table_part.astype(jnp.bfloat16)
    second_low = second_table_part.astype(jnp.bfloat16)
    count = particles.shape[0]
    width = L * L
    label_row = jnp.broadcast_to(group_ids.astype(jnp.bfloat16)[:, None], (count, 128))
    payload = jnp.concatenate([particles.reshape(count, width), label_row], axis=1)
    peers = lax.psum(1, "cls")
    gathered = lax.all_to_all(
        jnp.broadcast_to(payload, (peers,) + payload.shape[1:]), "cls", 0, 0, tiled=True
    )
    images = gathered[:, :width].reshape(-1, L, L)
    fourier_input = particle_band_rows(images, first_low, second_low)
    block_labels = gathered[:, width].astype(jnp.int32)
    rows = lax.psum(1, "dom")
    spread = jnp.broadcast_to(references[None], (rows,) + references.shape)
    pieces = lax.all_to_all(spread, "dom", 0, 0, tiled=True)
    maps = jnp.transpose(pieces, (1, 0, 2)).reshape(references.shape[0], -1)
    complete_input = lax.reduce_precision(fourier_input.astype(jnp.float32), 8, 7)
    contrast_transfer, noise_deviation = spectra(ctf_profile, noise_power, block_labels)
    abstract_value = (
        complete_input * (contrast_transfer / noise_deviation[None, :])[:, None, None, :]
    )
    output_value = complete_input * contrast_transfer[:, None, None, :]
    rbands = class_bands(maps, first_table_part, second_table_part)
    power = rbands[:, 0] ** 2 + rbands[:, 1] ** 2
    offset = 0.5 * jnp.dot(
        contrast_transfer * contrast_transfer / noise_deviation[None, :], power.T, precision=HIGHEST
    )
    peaks, totals, projs = class_step(abstract_value, output_value, rbands, offset.T, tabs)
    peaks, totals = lax.optimization_barrier((peaks, totals))
    local_top = jnp.max(peaks, axis=0)
    local_mass = jnp.sum(jnp.exp(peaks - local_top[None, :]) * totals, axis=0)
    own_summary = jnp.stack([local_top, local_mass])
    summary = lax.all_to_all(
        jnp.broadcast_to(own_summary[None], (peers,) + own_summary.shape), "cls", 0, 0, tiled=True
    )
    top = jnp.max(summary[:, 0], axis=0)
    mass = jnp.sum(jnp.exp(summary[:, 0] - top[None, :]) * summary[:, 1], axis=0)
    log_evidence = top + jnp.log(mass)
    share = jnp.exp(peaks - top[None, :]) / mass[None, :]
    numer = jnp.transpose(jnp.sum(share[:, :, None, None] * projs, axis=1), (1, 0, 2))
    weight = share * totals
    denom = jnp.sum(weight[:, :, None] * (contrast_transfer * contrast_transfer)[None], axis=1)
    stacked = jnp.concatenate([numer, denom[None]], axis=0)
    lanes = stacked.shape[2] // rows
    parts = jnp.moveaxis(stacked.reshape(3, stacked.shape[1], rows, lanes), 2, 0)
    owned = jnp.sum(lax.all_to_all(parts, "dom", 0, 0, tiled=True), axis=0)
    new_refs = owned[:2] / (owned[2] + 1.0)[None]
    return (new_refs, log_evidence)


def solution(mesh):
    in_specs = (P(("dom", "cls"), None, None), P(("dom", "cls")), P("cls", "dom"), P(), P())
    out_specs = (P(None, "cls", "dom"), P("dom"))
    return jax.shard_map(shards, mesh=mesh, in_specs=in_specs, out_specs=out_specs, check_vma=False)
```
